32 devices in a mesh: groups: 2 (over y), seq: 4 (over z), res: 2 (over x), chan: 2 (over core).
Axes of the slice: x: 2, y: 2, z: 4, core: 2. Of those that a mesh axis runs over, the one named last changes fastest.
Arguments:
- homolog_embedding: bfloat16 [2560, 64, 64], P(('groups', 'seq', 'chan'), 'res'), parts along dimension 0, may hold values from -6 to 6
- coupling_embedding: float32 [128, 64, 128], P(('groups', 'res'), ('seq', 'chan')), parts along dimension 0, may hold values from -6 to 6
- homolog_widen_weights: bfloat16 [64, 256], replicated, may hold values from -0.75 to 0.75
- homolog_shrink_weights: bfloat16 [256, 64], replicated, may hold values from -0.375 to 0.375
- lhs_projector: bfloat16 [64, 32], replicated, may hold values from -0.75 to 0.75
- rhs_projector: bfloat16 [64, 32], replicated, may hold values from -0.75 to 0.75
- moment_coupling_weights: float32 [1024, 128], replicated, may hold values from -6 to 6
- coupling_widen_weights: bfloat16 [128, 512], replicated, may hold values from -0.5 to 0.5
- coupling_shrink_weights: bfloat16 [512, 128], replicated, may hold values from -0.25 to 0.25
Outputs:
- homolog_refreshed: bfloat16 [2560, 64, 64], P(('groups', 'seq', 'chan'), 'res'), parts along dimension 0
- coupling_refreshed: float32 [128, 64, 128], P(('groups', 'res'), ('seq', 'chan')), parts along dimension 0
The draws below stay inside these ranges and needn't reach their ends.
There are 2 independent parts, one for each index of `groups`. The reference program is written for one: setup_inputs(seed, part) draws one part's arguments, and reference() takes and returns one part's arrays. A program takes and returns all parts, laid end to end along the dimension named above; an argument that names none is the same for every part. Nothing has to cross between parts.
All inputs are finite; a program needn't handle non-finite values.
Results may differ from the reference program's by a relative error of at most 0.0043.
Values may be sent and summed in bfloat16 or wider, within the bound.
No kernel may reach another device: no remote copies, remote signals or barrier semaphores. Data moves between devices by JAX's collectives and lax.ppermute only.
A program may use at most 64 MiB of HBM per device.

```python
import jax
import jax.numpy as jnp
from jax import lax

SUPPORT_LANES = 64
INNER_UNITS_SIZE = 256
PROJECTED_LANES = 32
COUPLING_LANES = 128
PH = 512
HOMOLOG_NUMBER = 1280
SITE_NUMBER = 64


def levels(key, dims, split, smallest, top_value):
    level, own = 1.0, jax.random.fold_in(key, 6)
    for dim, blocks in split:
        draws = jnp.exp(jax.random.uniform(jax.random.fold_in(own, dim), (blocks,), jnp.float32, smallest / len(split), top_value / len(split)))
        level = level * jnp.repeat(draws, dims[dim] // blocks).reshape([-1 if axis == dim else 1 for axis in range(len(dims))])
    return level


def scatter_about(stream_key, extent, width, reach, split=(), kind=jnp.bfloat16):
    loudness = levels(stream_key, extent, split, -0.22, 0.18) if split else 1.0
    drawn = jax.random.normal(stream_key, extent, jnp.float32) * width * loudness
    return jnp.minimum(jnp.maximum(drawn, -reach), reach).astype(kind)


def setup_inputs(seed: int = 0, part: int = 0) -> dict:
    key_of = jax.random.split(jax.random.key(seed), 10)
    part_keys = jax.random.split(jax.random.fold_in(key_of[9], part), 10)
    return {
        "homolog_embedding": scatter_about(part_keys[0], (HOMOLOG_NUMBER, SITE_NUMBER, SUPPORT_LANES), 1.0, 6.0, ((0, 8), (1, 2))),
        "coupling_embedding": scatter_about(part_keys[1], (SITE_NUMBER, SITE_NUMBER, COUPLING_LANES), 1.0, 6.0, ((0, 2), (1, 8)), jnp.float32),
        "homolog_widen_weights": scatter_about(key_of[2], (SUPPORT_LANES, INNER_UNITS_SIZE), SUPPORT_LANES ** -0.5, 0.75),
        "homolog_shrink_weights": scatter_about(key_of[3], (INNER_UNITS_SIZE, SUPPORT_LANES), INNER_UNITS_SIZE ** -0.5, 0.375),
        "lhs_projector": scatter_about(key_of[4], (SUPPORT_LANES, PROJECTED_LANES), SUPPORT_LANES ** -0.5, 0.75),
        "rhs_projector": scatter_about(key_of[5], (SUPPORT_LANES, PROJECTED_LANES), SUPPORT_LANES ** -0.5, 0.75),
        "moment_coupling_weights": scatter_about(key_of[6], (PROJECTED_LANES * PROJECTED_LANES, COUPLING_LANES), 1.0, 6.0, (), jnp.float32),
        "coupling_widen_weights": scatter_about(key_of[7], (COUPLING_LANES, PH), COUPLING_LANES ** -0.5, 0.5),
        "coupling_shrink_weights": scatter_about(key_of[8], (PH, COUPLING_LANES), PH ** -0.5, 0.25),
    }


def apply_layer_norm(values):
    mean = lax.optimization_barrier(jnp.mean(values, axis=-1, keepdims=True))
    centred = values - mean
    variance = lax.optimization_barrier(jnp.mean(centred * centred, axis=-1, keepdims=True))
    return centred * lax.rsqrt(variance + 1e-05)

def reference(homolog_embedding, coupling_embedding, homolog_widen_weights, homolog_shrink_weights, lhs_projector, rhs_projector, moment_coupling_weights, coupling_widen_weights, coupling_shrink_weights):
    cross_moment_average = homolog_embedding.reshape(HOMOLOG_NUMBER * SITE_NUMBER, SUPPORT_LANES)
    homolog_standardized = apply_layer_norm(cross_moment_average.astype(jnp.float32)).astype(jnp.bfloat16)
    homolog_inner_state = jnp.maximum(jnp.dot(homolog_standardized, homolog_widen_weights, preferred_element_type=jnp.float32), 0.0).astype(jnp.bfloat16)
    homolog_refreshed = (cross_moment_average.astype(jnp.float32) + jnp.dot(homolog_inner_state, homolog_shrink_weights, preferred_element_type=jnp.float32)).astype(jnp.bfloat16)
    alignment_normed2 = apply_layer_norm(homolog_refreshed.astype(jnp.float32)).astype(jnp.bfloat16)
    left_features = jnp.dot(alignment_normed2, lhs_projector, preferred_element_type=jnp.float32).astype(jnp.bfloat16).reshape(HOMOLOG_NUMBER, SITE_NUMBER, PROJECTED_LANES)
    right_features = jnp.dot(alignment_normed2, rhs_projector, preferred_element_type=jnp.float32).astype(jnp.bfloat16).reshape(HOMOLOG_NUMBER, SITE_NUMBER, PROJECTED_LANES)
    outer = jnp.einsum('sic,sje->ijce', left_features.astype(jnp.float32), right_features.astype(jnp.float32), precision=lax.Precision.HIGHEST) / HOMOLOG_NUMBER
    pair_update = jnp.dot(outer.reshape(SITE_NUMBER * SITE_NUMBER, PROJECTED_LANES * PROJECTED_LANES), moment_coupling_weights, precision=lax.Precision.HIGHEST, preferred_element_type=jnp.float32)
    pair_mid = coupling_embedding.reshape(SITE_NUMBER * SITE_NUMBER, COUPLING_LANES) + pair_update
    pair_norm = apply_layer_norm(pair_mid).astype(jnp.bfloat16)
    pair_hidden = jnp.maximum(jnp.dot(pair_norm, coupling_widen_weights, preferred_element_type=jnp.float32), 0.0).astype(jnp.bfloat16)
    coupling_refreshed = pair_mid + jnp.dot(pair_hidden, coupling_shrink_weights, preferred_element_type=jnp.float32)
    return (homolog_refreshed.reshape(HOMOLOG_NUMBER, SITE_NUMBER, SUPPORT_LANES), coupling_refreshed.reshape(SITE_NUMBER, SITE_NUMBER, COUPLING_LANES))
```

```python
import functools

import jax
import jax.numpy as jnp
from jax import lax
from jax.experimental import pallas as pl
from jax.experimental.pallas import tpu as pltpu
from jax.sharding import PartitionSpec as P


def apply_layer_norm(values):
    mean = jnp.mean(values, axis=-1, keepdims=True)
    centred = values - mean
    variance = jnp.mean(centred * centred, axis=-1, keepdims=True)
    return centred * lax.rsqrt(variance + 1e-05)


C_HI = 8
C_LO = 4
JB = 4


def outer_project_kernel(scale, lt_ref, r_ref, wh_ref, wl_ref, o_ref, vh_ref, vl_ref):
    width = wh_ref.shape[0] // (C_HI * C_LO)
    rows_i = lt_ref.shape[0] // (C_HI * C_LO)
    lanes = JB * width
    nja = r_ref.shape[1] // lanes
    dd = wh_ref.shape[1]

    @pl.when(pl.program_id(0) == 0)
    def _build():
        vh_ref[...] = jnp.zeros_like(vh_ref)
        vl_ref[...] = jnp.zeros_like(vl_ref)
        for c_hi in range(C_HI):
            for c_lo in range(C_LO):
                src = (c_hi * C_LO + c_lo) * width
                for jb in range(JB):
                    row = c_lo * lanes + jb * width
                    vh_ref[c_hi, row : row + width, jb * dd : (jb + 1) * dd] = wh_ref[src : src + width, :]
                    vl_ref[c_hi, row : row + width, jb * dd : (jb + 1) * dd] = wl_ref[src : src + width, :]

    def rearrange(y):
        return jnp.concatenate(
            [
                jnp.concatenate(
                    [y[c_lo * rows_i : (c_lo + 1) * rows_i, ja * lanes : (ja + 1) * lanes] for c_lo in range(C_LO)],
                    axis=1,
                )
                for ja in range(nja)
            ],
            axis=0,
        )

    acc = jnp.zeros(o_ref.shape, jnp.float32)
    block = C_LO * rows_i
    for c_hi in range(C_HI):
        x = jnp.dot(lt_ref[c_hi * block : (c_hi + 1) * block, :], r_ref[...], preferred_element_type=jnp.float32)
        xh = x.astype(jnp.bfloat16)
        xl = (x - xh.astype(jnp.float32)).astype(jnp.bfloat16)
        lh = rearrange(xh)
        ll = rearrange(xl)
        vh = vh_ref[c_hi]
        acc = acc + jnp.dot(lh, vh, preferred_element_type=jnp.float32)
        acc = acc + jnp.dot(ll, vh, preferred_element_type=jnp.float32)
        acc = acc + jnp.dot(lh, vl_ref[c_hi], preferred_element_type=jnp.float32)
    o_ref[...] = acc * scale


def outer_project(lt, r_all, wh, wl, scale):
    rows_i = lt.shape[0] // (C_HI * C_LO)
    width = wh.shape[0] // (C_HI * C_LO)
    lanes = JB * width
    total_lanes = r_all.shape[1]
    chunk = min(total_lanes, 16 * lanes)
    steps = total_lanes // chunk
    nja_chunk = chunk // lanes
    out_rows = (total_lanes // lanes) * rows_i
    d = wh.shape[1]
    s = lt.shape[1]
    flops = 2 * lt.shape[0] * s * total_lanes + 3 * 2 * out_rows * (C_LO * lanes) * (JB * d) * C_HI
    return pl.pallas_call(
        functools.partial(outer_project_kernel, scale),
        grid=(steps,),
        in_specs=[
            pl.BlockSpec(lt.shape, lambda q: (0, 0)),
            pl.BlockSpec((s, chunk), lambda q: (0, q)),
            pl.BlockSpec(wh.shape, lambda q: (0, 0)),
            pl.BlockSpec(wl.shape, lambda q: (0, 0)),
        ],
        out_specs=pl.BlockSpec((nja_chunk * rows_i, JB * d), lambda q: (q, 0)),
        out_shape=jax.ShapeDtypeStruct((out_rows, JB * d), jnp.float32),
        scratch_shapes=[
            pltpu.VMEM((C_HI, C_LO * lanes, JB * d), jnp.bfloat16),
            pltpu.VMEM((C_HI, C_LO * lanes, JB * d), jnp.bfloat16),
        ],
        compiler_params=pltpu.CompilerParams(
            dimension_semantics=("arbitrary",), vmem_limit_bytes=48 * 1024 * 1024
        ),
        cost_estimate=pl.CostEstimate(
            flops=flops,
            transcendentals=0,
            bytes_accessed=lt.size * 2 + r_all.size * 2 + wh.size * 4 + out_rows * JB * d * 4,
        ),
    )(lt, r_all, wh, wl)


def per_device(
    homolog_embedding,
    coupling_embedding,
    homolog_widen_weights,
    homolog_shrink_weights,
    lhs_projector,
    rhs_projector,
    moment_coupling_weights,
    coupling_widen_weights,
    coupling_shrink_weights,
):
    homologs_local_share, sites_local_share, homolog_lane_number = homolog_embedding.shape
    proj_width = lhs_projector.shape[1]
    pair_width = coupling_embedding.shape[2]
    cross_moment_average = homolog_embedding.reshape(
        homologs_local_share * sites_local_share, homolog_lane_number
    )
    homolog_standardized = apply_layer_norm(cross_moment_average.astype(jnp.float32)).astype(
        jnp.bfloat16
    )
    homolog_inner_state = jnp.maximum(
        jnp.dot(homolog_standardized, homolog_widen_weights, preferred_element_type=jnp.float32),
        0.0,
    ).astype(jnp.bfloat16)
    homolog_refreshed = (
        cross_moment_average.astype(jnp.float32)
        + jnp.dot(homolog_inner_state, homolog_shrink_weights, preferred_element_type=jnp.float32)
    ).astype(jnp.bfloat16)
    alignment_normed2 = apply_layer_norm(homolog_refreshed.astype(jnp.float32)).astype(jnp.bfloat16)
    left_features = (
        jnp.dot(alignment_normed2, lhs_projector, preferred_element_type=jnp.float32)
        .astype(jnp.bfloat16)
        .reshape(homologs_local_share, sites_local_share, proj_width)
    )
    right_features = (
        jnp.dot(alignment_normed2, rhs_projector, preferred_element_type=jnp.float32)
        .astype(jnp.bfloat16)
        .reshape(homologs_local_share, sites_local_share * proj_width)
    )
    owners = lax.axis_size(("seq", "chan"))
    depth_total = float(homologs_local_share * owners)
    block_cols = coupling_embedding.shape[1]

    lt = jnp.transpose(left_features, (2, 1, 0)).reshape(proj_width * sites_local_share, homologs_local_share)
    r_all = lax.all_gather(right_features, "res", axis=1, tiled=True)
    w_hi = moment_coupling_weights.astype(jnp.bfloat16)
    w_lo = (moment_coupling_weights - w_hi.astype(jnp.float32)).astype(jnp.bfloat16)
    partial_value = outer_project(lt, r_all, w_hi, w_lo, 1.0 / depth_total)
    pair_update = lax.psum_scatter(partial_value, ("seq", "chan"), scatter_dimension=0, tiled=True)
    nja_local = block_cols // JB
    pair_update = (
        pair_update.reshape(nja_local, sites_local_share, JB, pair_width)
        .transpose(1, 0, 2, 3)
        .reshape(sites_local_share * block_cols, pair_width)
    )
    pair_mid = coupling_embedding.reshape(sites_local_share * block_cols, pair_width) + pair_update
    pair_norm = apply_layer_norm(pair_mid).astype(jnp.bfloat16)
    pair_hidden = jnp.maximum(
        jnp.dot(pair_norm, coupling_widen_weights, preferred_element_type=jnp.float32), 0.0
    ).astype(jnp.bfloat16)
    coupling_refreshed = pair_mid + jnp.dot(
        pair_hidden, coupling_shrink_weights, preferred_element_type=jnp.float32
    )
    return (
        homolog_refreshed.reshape(homologs_local_share, sites_local_share, homolog_lane_number),
        coupling_refreshed.reshape(sites_local_share, block_cols, pair_width),
    )


def solution(mesh):
    return jax.shard_map(
        per_device,
        mesh=mesh,
        in_specs=(
            P(("groups", "seq", "chan"), "res", None),
            P(("groups", "res"), ("seq", "chan"), None),
            P(),
            P(),
            P(),
            P(),
            P(),
            P(),
            P(),
        ),
        out_specs=(
            P(("groups", "seq", "chan"), "res", None),
            P(("groups", "res"), ("seq", "chan"), None),
        ),
        check_vma=False,
    )
```

```python
import functools

import jax
import jax.numpy as jnp
from jax import lax
from jax.experimental import pallas as pl
from jax.experimental.pallas import tpu as pltpu
from jax.sharding import PartitionSpec as P


def apply_layer_norm(values):
    mean = jnp.mean(values, axis=-1, keepdims=True)
    centred = values - mean
    variance = jnp.mean(centred * centred, axis=-1, keepdims=True)
    return centred * lax.rsqrt(variance + 1e-05)


C_HI = 8
C_LO = 4
JB = 4


def outer_project_kernel(scale, lt_ref, r_ref, wh_ref, wl_ref, o_ref, vh_ref, vl_ref):
    width = wh_ref.shape[0] // (C_HI * C_LO)
    rows_i = lt_ref.shape[0] // (C_HI * C_LO)
    lanes = JB * width
    nja = r_ref.shape[1] // lanes
    dd = wh_ref.shape[1]

    @pl.when(pl.program_id(0) == 0)
    def _build():
        vh_ref[...] = jnp.zeros_like(vh_ref)
        vl_ref[...] = jnp.zeros_like(vl_ref)
        for c_hi in range(C_HI):
            for c_lo in range(C_LO):
                src = (c_hi * C_LO + c_lo) * width
                for jb in range(JB):
                    row = c_lo * lanes + jb * width
                    vh_ref[c_hi, row : row + width, jb * dd : (jb + 1) * dd] = wh_ref[src : src + width, :]
                    vl_ref[c_hi, row : row + width, jb * dd : (jb + 1) * dd] = wl_ref[src : src + width, :]

    def rearrange(y):
        return jnp.concatenate(
            [
                jnp.concatenate(
                    [y[c_lo * rows_i : (c_lo + 1) * rows_i, ja * lanes : (ja + 1) * lanes] for c_lo in range(C_LO)],
                    axis=1,
                )
                for ja in range(nja)
            ],
            axis=0,
        )

    acc = jnp.zeros(o_ref.shape, jnp.float32)
    block = C_LO * rows_i
    for c_hi in range(C_HI):
        x = jnp.dot(lt_ref[c_hi * block : (c_hi + 1) * block, :], r_ref[...], preferred_element_type=jnp.float32)
        xh = x.astype(jnp.bfloat16)
        xl = (x - xh.astype(jnp.float32)).astype(jnp.bfloat16)
        lh = rearrange(xh)
        ll = rearrange(xl)
        vh = vh_ref[c_hi]
        acc = acc + jnp.dot(lh, vh, preferred_element_type=jnp.float32)
        acc = acc + jnp.dot(ll, vh, preferred_element_type=jnp.float32)
        acc = acc + jnp.dot(lh, vl_ref[c_hi], preferred_element_type=jnp.float32)
    o_ref[...] = acc * scale


def outer_project(lt, r_all, wh, wl, scale):
    rows_i = lt.shape[0] // (C_HI * C_LO)
    width = wh.shape[0] // (C_HI * C_LO)
    lanes = JB * width
    total_lanes = r_all.shape[1]
    chunk = min(total_lanes, 16 * lanes)
    steps = total_lanes // chunk
    nja_chunk = chunk // lanes
    out_rows = (total_lanes // lanes) * rows_i
    d = wh.shape[1]
    s = lt.shape[1]
    flops = 2 * lt.shape[0] * s * total_lanes + 3 * 2 * out_rows * (C_LO * lanes) * (JB * d) * C_HI
    return pl.pallas_call(
        functools.partial(outer_project_kernel, scale),
        grid=(steps,),
        in_specs=[
            pl.BlockSpec(lt.shape, lambda q: (0, 0)),
            pl.BlockSpec((s, chunk), lambda q: (0, q)),
            pl.BlockSpec(wh.shape, lambda q: (0, 0)),
            pl.BlockSpec(wl.shape, lambda q: (0, 0)),
        ],
        out_specs=pl.BlockSpec((nja_chunk * rows_i, JB * d), lambda q: (q, 0)),
        out_shape=jax.ShapeDtypeStruct((out_rows, JB * d), jnp.float32),
        scratch_shapes=[
            pltpu.VMEM((C_HI, C_LO * lanes, JB * d), jnp.bfloat16),
            pltpu.VMEM((C_HI, C_LO * lanes, JB * d), jnp.bfloat16),
        ],
        compiler_params=pltpu.CompilerParams(
            dimension_semantics=("arbitrary",), vmem_limit_bytes=48 * 1024 * 1024
        ),
        cost_estimate=pl.CostEstimate(
            flops=flops,
            transcendentals=0,
            bytes_accessed=lt.size * 2 + r_all.size * 2 + wh.size * 4 + out_rows * JB * d * 4,
        ),
    )(lt, r_all, wh, wl)


def reduce_over_sequences(partial_value):
    nseq = lax.axis_size("seq")
    nchan = lax.axis_size("chan")
    if nchan != 2:
        return lax.psum_scatter(partial_value, ("seq", "chan"), scatter_dimension=0, tiled=True)
    rows, cols = partial_value.shape
    chunk = rows // (nseq * nchan)
    xs = partial_value.reshape(nseq, nchan, chunk, cols)
    c = lax.axis_index("chan")
    mine = lax.dynamic_index_in_dim(xs, c, axis=1, keepdims=False)
    other = lax.dynamic_index_in_dim(xs, 1 - c, axis=1, keepdims=False)
    received = lax.ppermute(other, "chan", [(0, 1), (1, 0)])
    part = mine + received
    gathered = lax.all_to_all(part, "seq", 0, 0, tiled=False)
    return gathered.sum(axis=0)


def per_device(
    homolog_embedding,
    coupling_embedding,
    homolog_widen_weights,
    homolog_shrink_weights,
    lhs_projector,
    rhs_projector,
    moment_coupling_weights,
    coupling_widen_weights,
    coupling_shrink_weights,
):
    homologs_local_share, sites_local_share, homolog_lane_number = homolog_embedding.shape
    proj_width = lhs_projector.shape[1]
    pair_width = coupling_embedding.shape[2]
    cross_moment_average = homolog_embedding.reshape(
        homologs_local_share * sites_local_share, homolog_lane_number
    )
    homolog_standardized = apply_layer_norm(cross_moment_average.astype(jnp.float32)).astype(
        jnp.bfloat16
    )
    homolog_inner_state = jnp.maximum(
        jnp.dot(homolog_standardized, homolog_widen_weights, preferred_element_type=jnp.float32),
        0.0,
    ).astype(jnp.bfloat16)
    homolog_refreshed = (
        cross_moment_average.astype(jnp.float32)
        + jnp.dot(homolog_inner_state, homolog_shrink_weights, preferred_element_type=jnp.float32)
    ).astype(jnp.bfloat16)
    alignment_normed2 = apply_layer_norm(homolog_refreshed.astype(jnp.float32)).astype(jnp.bfloat16)
    left_features = (
        jnp.dot(alignment_normed2, lhs_projector, preferred_element_type=jnp.float32)
        .astype(jnp.bfloat16)
        .reshape(homologs_local_share, sites_local_share, proj_width)
    )
    right_features = (
        jnp.dot(alignment_normed2, rhs_projector, preferred_element_type=jnp.float32)
        .astype(jnp.bfloat16)
        .reshape(homologs_local_share, sites_local_share * proj_width)
    )
    owners = lax.axis_size(("seq", "chan"))
    depth_total = float(homologs_local_share * owners)
    block_cols = coupling_embedding.shape[1]

    lt = jnp.transpose(left_features, (2, 1, 0)).reshape(proj_width * sites_local_share, homologs_local_share)
    r_all = lax.all_gather(right_features, "res", axis=1, tiled=True)
    w_hi_f32 = lax.reduce_precision(moment_coupling_weights, exponent_bits=8, mantissa_bits=7)
    w_hi = w_hi_f32.astype(jnp.bfloat16)
    w_lo = (moment_coupling_weights - w_hi_f32).astype(jnp.bfloat16)
    partial_value = outer_project(lt, r_all, w_hi, w_lo, 1.0 / depth_total)
    pair_update = reduce_over_sequences(partial_value)
    nja_local = block_cols // JB
    pair_update = (
        pair_update.reshape(nja_local, sites_local_share, JB, pair_width)
        .transpose(1, 0, 2, 3)
        .reshape(sites_local_share * block_cols, pair_width)
    )
    pair_mid = coupling_embedding.reshape(sites_local_share * block_cols, pair_width) + pair_update
    pair_norm = apply_layer_norm(pair_mid).astype(jnp.bfloat16)
    pair_hidden = jnp.maximum(
        jnp.dot(pair_norm, coupling_widen_weights, preferred_element_type=jnp.float32), 0.0
    ).astype(jnp.bfloat16)
    coupling_refreshed = pair_mid + jnp.dot(
        pair_hidden, coupling_shrink_weights, preferred_element_type=jnp.float32
    )
    return (
        homolog_refreshed.reshape(homologs_local_share, sites_local_share, homolog_lane_number),
        coupling_refreshed.reshape(sites_local_share, block_cols, pair_width),
    )


def solution(mesh):
    return jax.shard_map(
        per_device,
        mesh=mesh,
        in_specs=(
            P(("groups", "seq", "chan"), "res", None),
            P(("groups", "res"), ("seq", "chan"), None),
            P(),
            P(),
            P(),
            P(),
            P(),
            P(),
            P(),
        ),
        out_specs=(
            P(("groups", "seq", "chan"), "res", None),
            P(("groups", "res"), ("seq", "chan"), None),
        ),
        check_vma=False,
    )
```

```python
import functools

import jax
import jax.numpy as jnp
from jax import lax
from jax.experimental import pallas as pl
from jax.experimental.pallas import tpu as pltpu
from jax.sharding import PartitionSpec as P


def apply_layer_norm(values):
    mean = jnp.mean(values, axis=-1, keepdims=True)
    centred = values - mean
    variance = jnp.mean(centred * centred, axis=-1, keepdims=True)
    return centred * lax.rsqrt(variance + 1e-05)


C_HI = 8
C_LO = 4
JB = 4


def outer_project_kernel(scale, lt_ref, r_ref, wh_ref, wl_ref, o_ref, vh_ref, vl_ref):
    width = wh_ref.shape[0] // (C_HI * C_LO)
    rows_i = lt_ref.shape[0] // (C_HI * C_LO)
    lanes = JB * width
    nja = r_ref.shape[0] // lanes
    dd = wh_ref.shape[1]

    @pl.when(pl.program_id(0) == 0)
    def _build():
        vh_ref[...] = jnp.zeros_like(vh_ref)
        vl_ref[...] = jnp.zeros_like(vl_ref)
        for c_hi in range(C_HI):
            for c_lo in range(C_LO):
                src = (c_hi * C_LO + c_lo) * width
                for jb in range(JB):
                    row = c_lo * lanes + jb * width
                    vh_ref[c_hi, row : row + width, jb * dd : (jb + 1) * dd] = wh_ref[src : src + width, :]
                    vl_ref[c_hi, row : row + width, jb * dd : (jb + 1) * dd] = wl_ref[src : src + width, :]

    def rearrange(y):
        return jnp.concatenate(
            [
                jnp.concatenate(
                    [y[c_lo * rows_i : (c_lo + 1) * rows_i, ja * lanes : (ja + 1) * lanes] for c_lo in range(C_LO)],
                    axis=1,
                )
                for ja in range(nja)
            ],
            axis=0,
        )

    acc = jnp.zeros(o_ref.shape, jnp.float32)
    block = C_LO * rows_i
    for c_hi in range(C_HI):
        x = lax.dot_general(
            lt_ref[c_hi * block : (c_hi + 1) * block, :].astype(jnp.bfloat16),
            r_ref[...],
            (((1,), (1,)), ((), ())),
            preferred_element_type=jnp.float32,
        )
        xh = x.astype(jnp.bfloat16)
        xl = (x - xh.astype(jnp.float32)).astype(jnp.bfloat16)
        lh = rearrange(xh)
        ll = rearrange(xl)
        vh = vh_ref[c_hi]
        acc = acc + jnp.dot(lh, vh, preferred_element_type=jnp.float32)
        acc = acc + jnp.dot(ll, vh, preferred_element_type=jnp.float32)
        acc = acc + jnp.dot(lh, vl_ref[c_hi], preferred_element_type=jnp.float32)
    o_ref[...] = acc * scale


def outer_project(lt, r_all, wh, wl, scale):
    rows_i = lt.shape[0] // (C_HI * C_LO)
    width = wh.shape[0] // (C_HI * C_LO)
    lanes = JB * width
    total_lanes = r_all.shape[0]
    chunk = min(total_lanes, 16 * lanes)
    steps = total_lanes // chunk
    nja_chunk = chunk // lanes
    out_rows = (total_lanes // lanes) * rows_i
    d = wh.shape[1]
    s = lt.shape[1]
    flops = 2 * lt.shape[0] * s * total_lanes + 3 * 2 * out_rows * (C_LO * lanes) * (JB * d) * C_HI
    return pl.pallas_call(
        functools.partial(outer_project_kernel, scale),
        grid=(steps,),
        in_specs=[
            pl.BlockSpec(lt.shape, lambda q: (0, 0)),
            pl.BlockSpec((chunk, s), lambda q: (q, 0)),
            pl.BlockSpec(wh.shape, lambda q: (0, 0)),
            pl.BlockSpec(wl.shape, lambda q: (0, 0)),
        ],
        out_specs=pl.BlockSpec((nja_chunk * rows_i, JB * d), lambda q: (q, 0)),
        out_shape=jax.ShapeDtypeStruct((out_rows, JB * d), jnp.float32),
        scratch_shapes=[
            pltpu.VMEM((C_HI, C_LO * lanes, JB * d), jnp.bfloat16),
            pltpu.VMEM((C_HI, C_LO * lanes, JB * d), jnp.bfloat16),
        ],
        compiler_params=pltpu.CompilerParams(
            dimension_semantics=("arbitrary",), vmem_limit_bytes=48 * 1024 * 1024
        ),
        cost_estimate=pl.CostEstimate(
            flops=flops,
            transcendentals=0,
            bytes_accessed=lt.size * 4 + r_all.size * 2 + wh.size * 4 + out_rows * JB * d * 4,
        ),
    )(lt, r_all, wh, wl)


def msa_kernel(x_ref, ww_ref, ws_ref, pt_ref, o_ref, lt_ref, rt_ref, n2_ref):
    x = x_ref[...].astype(jnp.float32)
    n1 = apply_layer_norm(x).astype(jnp.bfloat16)
    hidden = jnp.maximum(jnp.dot(n1, ww_ref[...], preferred_element_type=jnp.float32), 0.0).astype(jnp.bfloat16)
    refreshed = (x + jnp.dot(hidden, ws_ref[...], preferred_element_type=jnp.float32)).astype(jnp.bfloat16)
    o_ref[...] = refreshed
    k = x_ref.shape[1]
    n2_ref[:, :k] = apply_layer_norm(refreshed.astype(jnp.float32)).astype(jnp.bfloat16).astype(jnp.float32)
    n2_ref[:, k:] = jnp.zeros((n2_ref.shape[0], n2_ref.shape[1] - k), jnp.float32)
    width = pt_ref.shape[0] // 2
    sites = rt_ref.shape[0] // width
    depth = rt_ref.shape[1]
    pt = pt_ref[...]

    def body(i, carry):
        rows = n2_ref[pl.ds(i, depth, stride=sites), :].astype(jnp.bfloat16)
        proj = lax.dot_general(pt, rows, (((1,), (1,)), ((), ())), preferred_element_type=jnp.float32)
        start = pl.multiple_of(i * width, width)
        lt_ref[pl.ds(start, width), :] = proj[:width]
        rt_ref[pl.ds(start, width), :] = proj[width:].astype(jnp.bfloat16)
        return carry

    lax.fori_loop(0, sites, body, 0)


def msa_block(x2, ww, ws, pt, depth, sites):
    rows, k = x2.shape
    width = pt.shape[0] // 2
    hidden = ww.shape[1]
    return pl.pallas_call(
        msa_kernel,
        out_shape=(
            jax.ShapeDtypeStruct((rows, k), jnp.bfloat16),
            jax.ShapeDtypeStruct((width * sites, depth), jnp.float32),
            jax.ShapeDtypeStruct((sites * width, depth), jnp.bfloat16),
        ),
        in_specs=[pl.BlockSpec(memory_space=pltpu.VMEM)] * 4,
        out_specs=(pl.BlockSpec(memory_space=pltpu.VMEM),) * 3,
        scratch_shapes=[pltpu.VMEM((rows, pt.shape[1]), jnp.float32)],
        compiler_params=pltpu.CompilerParams(vmem_limit_bytes=48 * 1024 * 1024),
        cost_estimate=pl.CostEstimate(
            flops=2 * rows * k * hidden * 2 + 2 * rows * k * 2 * width,
            transcendentals=2 * rows,
            bytes_accessed=rows * k * 4 + 2 * rows * width * 3,
        ),
    )(x2, ww, ws, pt)


def reduce_over_sequences(partial_value):
    nseq = lax.axis_size("seq")
    nchan = lax.axis_size("chan")
    if nchan != 2:
        return lax.psum_scatter(partial_value, ("seq", "chan"), scatter_dimension=0, tiled=True)
    rows, cols = partial_value.shape
    chunk = rows // (nseq * nchan)
    xs = partial_value.reshape(nseq, nchan, chunk, cols)
    c = lax.axis_index("chan")
    mine = lax.dynamic_index_in_dim(xs, c, axis=1, keepdims=False)
    other = lax.dynamic_index_in_dim(xs, 1 - c, axis=1, keepdims=False)
    received = lax.ppermute(other, "chan", [(0, 1), (1, 0)])
    part = mine + received
    gathered = lax.all_to_all(part, "seq", 0, 0, tiled=False)
    return gathered.sum(axis=0)


def per_device(
    homolog_embedding,
    coupling_embedding,
    homolog_widen_weights,
    homolog_shrink_weights,
    lhs_projector,
    rhs_projector,
    moment_coupling_weights,
    coupling_widen_weights,
    coupling_shrink_weights,
):
    homologs_local_share, sites_local_share, homolog_lane_number = homolog_embedding.shape
    proj_width = lhs_projector.shape[1]
    pair_width = coupling_embedding.shape[2]
    x2 = homolog_embedding.reshape(homologs_local_share * sites_local_share, homolog_lane_number)
    pt = jnp.concatenate([lhs_projector, rhs_projector], axis=1).T
    pt = jnp.pad(pt, ((0, 0), (0, 128 - homolog_lane_number)))
    homolog_refreshed, left_t, right_t = msa_block(
        x2, homolog_widen_weights, homolog_shrink_weights, pt, homologs_local_share, sites_local_share
    )
    lt = (
        left_t.reshape(sites_local_share, proj_width, homologs_local_share)
        .transpose(1, 0, 2)
        .reshape(proj_width * sites_local_share, homologs_local_share)
    )
    owners = lax.axis_size(("seq", "chan"))
    depth_total = float(homologs_local_share * owners)
    block_cols = coupling_embedding.shape[1]

    r_all = lax.all_gather(right_t, "res", axis=0, tiled=True)
    w_hi_f32 = lax.reduce_precision(moment_coupling_weights, exponent_bits=8, mantissa_bits=7)
    w_hi = w_hi_f32.astype(jnp.bfloat16)
    w_lo = (moment_coupling_weights - w_hi_f32).astype(jnp.bfloat16)
    partial_value = outer_project(lt, r_all, w_hi, w_lo, 1.0 / depth_total)
    pair_update = reduce_over_sequences(partial_value)
    nja_local = block_cols // JB
    pair_update = (
        pair_update.reshape(nja_local, sites_local_share, JB, pair_width)
        .transpose(1, 0, 2, 3)
        .reshape(sites_local_share * block_cols, pair_width)
    )
    pair_mid = coupling_embedding.reshape(sites_local_share * block_cols, pair_width) + pair_update
    pair_norm = apply_layer_norm(pair_mid).astype(jnp.bfloat16)
    pair_hidden = jnp.maximum(
        jnp.dot(pair_norm, coupling_widen_weights, preferred_element_type=jnp.float32), 0.0
    ).astype(jnp.bfloat16)
    coupling_refreshed = pair_mid + jnp.dot(
        pair_hidden, coupling_shrink_weights, preferred_element_type=jnp.float32
    )
    return (
        homolog_refreshed.reshape(homologs_local_share, sites_local_share, homolog_lane_number),
        coupling_refreshed.reshape(sites_local_share, block_cols, pair_width),
    )


def solution(mesh):
    return jax.shard_map(
        per_device,
        mesh=mesh,
        in_specs=(
            P(("groups", "seq", "chan"), "res", None),
            P(("groups", "res"), ("seq", "chan"), None),
            P(),
            P(),
            P(),
            P(),
            P(),
            P(),
            P(),
        ),
        out_specs=(
            P(("groups", "seq", "chan"), "res", None),
            P(("groups", "res"), ("seq", "chan"), None),
        ),
        check_vma=False,
    )
```

```python
import functools

import jax
import jax.numpy as jnp
from jax import lax
from jax.experimental import pallas as pl
from jax.experimental.pallas import tpu as pltpu
from jax.sharding import PartitionSpec as P


def apply_layer_norm(values):
    mean = jnp.mean(values, axis=-1, keepdims=True)
    centred = values - mean
    variance = jnp.mean(centred * centred, axis=-1, keepdims=True)
    return centred * lax.rsqrt(variance + 1e-05)


C_HI = 8
C_LO = 4
JB = 4


def outer_project_kernel(scale, lt_ref, r_ref, wh_ref, wl_ref, o_ref, vh_ref, vl_ref):
    width = wh_ref.shape[0] // (C_HI * C_LO)
    rows_i = lt_ref.shape[0] // (C_HI * C_LO)
    lanes = JB * width
    nja = r_ref.shape[1] // lanes
    dd = wh_ref.shape[1]

    @pl.when(pl.program_id(0) == 0)
    def _build():
        vh_ref[...] = jnp.zeros_like(vh_ref)
        vl_ref[...] = jnp.zeros_like(vl_ref)
        for c_hi in range(C_HI):
            for c_lo in range(C_LO):
                src = (c_hi * C_LO + c_lo) * width
                for jb in range(JB):
                    row = c_lo * lanes + jb * width
                    vh_ref[c_hi, row : row + width, jb * dd : (jb + 1) * dd] = wh_ref[src : src + width, :]
                    vl_ref[c_hi, row : row + width, jb * dd : (jb + 1) * dd] = wl_ref[src : src + width, :]

    def rearrange(y):
        return jnp.concatenate(
            [
                jnp.concatenate(
                    [y[c_lo * rows_i : (c_lo + 1) * rows_i, ja * lanes : (ja + 1) * lanes] for c_lo in range(C_LO)],
                    axis=1,
                )
                for ja in range(nja)
            ],
            axis=0,
        )

    acc = jnp.zeros(o_ref.shape, jnp.float32)
    block = C_LO * rows_i
    for c_hi in range(C_HI):
        x = jnp.dot(lt_ref[c_hi * block : (c_hi + 1) * block, :], r_ref[...], preferred_element_type=jnp.float32)
        xh = x.astype(jnp.bfloat16)
        xl = (x - xh.astype(jnp.float32)).astype(jnp.bfloat16)
        lh = rearrange(xh)
        ll = rearrange(xl)
        vh = vh_ref[c_hi]
        acc = acc + jnp.dot(lh, vh, preferred_element_type=jnp.float32)
        acc = acc + jnp.dot(ll, vh, preferred_element_type=jnp.float32)
        acc = acc + jnp.dot(lh, vl_ref[c_hi], preferred_element_type=jnp.float32)
    o_ref[...] = acc * scale


def outer_project(lt, r_all, wh, wl, scale):
    rows_i = lt.shape[0] // (C_HI * C_LO)
    width = wh.shape[0] // (C_HI * C_LO)
    lanes = JB * width
    total_lanes = r_all.shape[1]
    chunk = min(total_lanes, 16 * lanes)
    steps = total_lanes // chunk
    nja_chunk = chunk // lanes
    out_rows = (total_lanes // lanes) * rows_i
    d = wh.shape[1]
    s = lt.shape[1]
    flops = 2 * lt.shape[0] * s * total_lanes + 3 * 2 * out_rows * (C_LO * lanes) * (JB * d) * C_HI
    return pl.pallas_call(
        functools.partial(outer_project_kernel, scale),
        grid=(steps,),
        in_specs=[
            pl.BlockSpec(lt.shape, lambda q: (0, 0)),
            pl.BlockSpec((s, chunk), lambda q: (0, q)),
            pl.BlockSpec(wh.shape, lambda q: (0, 0)),
            pl.BlockSpec(wl.shape, lambda q: (0, 0)),
        ],
        out_specs=pl.BlockSpec((nja_chunk * rows_i, JB * d), lambda q: (q, 0)),
        out_shape=jax.ShapeDtypeStruct((out_rows, JB * d), jnp.float32),
        scratch_shapes=[
            pltpu.VMEM((C_HI, C_LO * lanes, JB * d), jnp.bfloat16),
            pltpu.VMEM((C_HI, C_LO * lanes, JB * d), jnp.bfloat16),
        ],
        compiler_params=pltpu.CompilerParams(
            dimension_semantics=("arbitrary",), vmem_limit_bytes=48 * 1024 * 1024
        ),
        cost_estimate=pl.CostEstimate(
            flops=flops,
            transcendentals=0,
            bytes_accessed=lt.size * 2 + r_all.size * 2 + wh.size * 4 + out_rows * JB * d * 4,
        ),
    )(lt, r_all, wh, wl)


def reduce_over_sequences(partial_value):
    nseq = lax.axis_size("seq")
    nchan = lax.axis_size("chan")
    if nchan != 2:
        return lax.psum_scatter(partial_value, ("seq", "chan"), scatter_dimension=0, tiled=True)
    rows, cols = partial_value.shape
    chunk = rows // (nseq * nchan)
    xs = partial_value.reshape(nseq, nchan, chunk, cols)
    c = lax.axis_index("chan")
    mine = lax.dynamic_index_in_dim(xs, c, axis=1, keepdims=False)
    other = lax.dynamic_index_in_dim(xs, 1 - c, axis=1, keepdims=False)
    received = lax.ppermute(other, "chan", [(0, 1), (1, 0)])
    part = mine + received
    if nseq > 4:
        gathered = lax.all_to_all(part, "seq", 0, 0, tiled=False)
        return gathered.sum(axis=0)
    me = lax.axis_index("seq")
    acc = lax.dynamic_index_in_dim(part, me, axis=0, keepdims=False)
    for k in range(1, nseq):
        src = lax.dynamic_index_in_dim(part, (me + k) % nseq, axis=0, keepdims=False)
        acc = acc + lax.ppermute(src, "seq", [(q, (q + k) % nseq) for q in range(nseq)])
    return acc


def per_device(
    homolog_embedding,
    coupling_embedding,
    homolog_widen_weights,
    homolog_shrink_weights,
    lhs_projector,
    rhs_projector,
    moment_coupling_weights,
    coupling_widen_weights,
    coupling_shrink_weights,
):
    homologs_local_share, sites_local_share, homolog_lane_number = homolog_embedding.shape
    proj_width = lhs_projector.shape[1]
    pair_width = coupling_embedding.shape[2]
    cross_moment_average = homolog_embedding.reshape(
        homologs_local_share * sites_local_share, homolog_lane_number
    )
    homolog_standardized = apply_layer_norm(cross_moment_average.astype(jnp.float32)).astype(
        jnp.bfloat16
    )
    homolog_inner_state = jnp.maximum(
        jnp.dot(homolog_standardized, homolog_widen_weights, preferred_element_type=jnp.float32),
        0.0,
    ).astype(jnp.bfloat16)
    homolog_refreshed = (
        cross_moment_average.astype(jnp.float32)
        + jnp.dot(homolog_inner_state, homolog_shrink_weights, preferred_element_type=jnp.float32)
    ).astype(jnp.bfloat16)
    alignment_normed2 = apply_layer_norm(homolog_refreshed.astype(jnp.float32)).astype(jnp.bfloat16)
    left_features = (
        jnp.dot(alignment_normed2, lhs_projector, preferred_element_type=jnp.float32)
        .astype(jnp.bfloat16)
        .reshape(homologs_local_share, sites_local_share, proj_width)
    )
    right_features = (
        jnp.dot(alignment_normed2, rhs_projector, preferred_element_type=jnp.float32)
        .astype(jnp.bfloat16)
        .reshape(homologs_local_share, sites_local_share * proj_width)
    )
    owners = lax.axis_size(("seq", "chan"))
    depth_total = float(homologs_local_share * owners)
    block_cols = coupling_embedding.shape[1]

    lt = jnp.transpose(left_features, (2, 1, 0)).reshape(proj_width * sites_local_share, homologs_local_share)
    w_hi_f32 = lax.reduce_precision(moment_coupling_weights, exponent_bits=8, mantissa_bits=7)
    w_hi = w_hi_f32.astype(jnp.bfloat16)
    w_lo = (moment_coupling_weights - w_hi_f32).astype(jnp.bfloat16)
    nres = lax.axis_size("res")
    if nres == 2:
        r_other = lax.ppermute(right_features, "res", [(0, 1), (1, 0)])
        p_own = outer_project(lt, right_features, w_hi, w_lo, 1.0 / depth_total)
        p_other = outer_project(lt, r_other, w_hi, w_lo, 1.0 / depth_total)
        first = lax.axis_index("res") == 0
        partial_value = jnp.where(
            first, jnp.concatenate([p_own, p_other], axis=0), jnp.concatenate([p_other, p_own], axis=0)
        )
    else:
        r_all = lax.all_gather(right_features, "res", axis=1, tiled=True)
        partial_value = outer_project(lt, r_all, w_hi, w_lo, 1.0 / depth_total)
    pair_update = reduce_over_sequences(partial_value)
    nja_local = block_cols // JB
    pair_update = (
        pair_update.reshape(nja_local, sites_local_share, JB, pair_width)
        .transpose(1, 0, 2, 3)
        .reshape(sites_local_share * block_cols, pair_width)
    )
    pair_mid = coupling_embedding.reshape(sites_local_share * block_cols, pair_width) + pair_update
    pair_norm = apply_layer_norm(pair_mid).astype(jnp.bfloat16)
    pair_hidden = jnp.maximum(
        jnp.dot(pair_norm, coupling_widen_weights, preferred_element_type=jnp.float32), 0.0
    ).astype(jnp.bfloat16)
    coupling_refreshed = pair_mid + jnp.dot(
        pair_hidden, coupling_shrink_weights, preferred_element_type=jnp.float32
    )
    return (
        homolog_refreshed.reshape(homologs_local_share, sites_local_share, homolog_lane_number),
        coupling_refreshed.reshape(sites_local_share, block_cols, pair_width),
    )


def solution(mesh):
    return jax.shard_map(
        per_device,
        mesh=mesh,
        in_specs=(
            P(("groups", "seq", "chan"), "res", None),
            P(("groups", "res"), ("seq", "chan"), None),
            P(),
            P(),
            P(),
            P(),
            P(),
            P(),
            P(),
        ),
        out_specs=(
            P(("groups", "seq", "chan"), "res", None),
            P(("groups", "res"), ("seq", "chan"), None),
        ),
        check_vma=False,
    )
```

```python
import functools

import jax
import jax.numpy as jnp
from jax import lax
from jax.experimental import pallas as pl
from jax.experimental.pallas import tpu as pltpu
from jax.sharding import PartitionSpec as P


def apply_layer_norm(values):
    mean = jnp.mean(values, axis=-1, keepdims=True)
    centred = values - mean
    variance = jnp.mean(centred * centred, axis=-1, keepdims=True)
    return centred * lax.rsqrt(variance + 1e-05)


C_HI = 8
C_LO = 4
JB = 4


def outer_project_kernel(scale, lt_ref, r_ref, wh_ref, wl_ref, o_ref, vh_ref, vl_ref):
    width = wh_ref.shape[0] // (C_HI * C_LO)
    rows_i = lt_ref.shape[0] // (C_HI * C_LO)
    lanes = JB * width
    nja = r_ref.shape[1] // lanes
    dd = wh_ref.shape[1]

    @pl.when(pl.program_id(0) == 0)
    def _build():
        vh_ref[...] = jnp.zeros_like(vh_ref)
        vl_ref[...] = jnp.zeros_like(vl_ref)
        for c_hi in range(C_HI):
            for c_lo in range(C_LO):
                src = (c_hi * C_LO + c_lo) * width
                for jb in range(JB):
                    row = c_lo * lanes + jb * width
                    vh_ref[c_hi, row : row + width, jb * dd : (jb + 1) * dd] = wh_ref[src : src + width, :]
                    vl_ref[c_hi, row : row + width, jb * dd : (jb + 1) * dd] = wl_ref[src : src + width, :]

    def rearrange(y):
        return jnp.concatenate(
            [
                jnp.concatenate(
                    [y[c_lo * rows_i : (c_lo + 1) * rows_i, ja * lanes : (ja + 1) * lanes] for c_lo in range(C_LO)],
                    axis=1,
                )
                for ja in range(nja)
            ],
            axis=0,
        )

    acc = jnp.zeros(o_ref.shape, jnp.float32)
    block = C_LO * rows_i
    for c_hi in range(C_HI):
        x = jnp.dot(lt_ref[c_hi * block : (c_hi + 1) * block, :], r_ref[...], preferred_element_type=jnp.float32)
        xh = x.astype(jnp.bfloat16)
        xl = (x - xh.astype(jnp.float32)).astype(jnp.bfloat16)
        lh = rearrange(xh)
        ll = rearrange(xl)
        vh = vh_ref[c_hi]
        acc = acc + jnp.dot(lh, vh, preferred_element_type=jnp.float32)
        acc = acc + jnp.dot(ll, vh, preferred_element_type=jnp.float32)
        acc = acc + jnp.dot(lh, vl_ref[c_hi], preferred_element_type=jnp.float32)
    o_ref[...] = acc * scale


def outer_project(lt, r_all, wh, wl, scale):
    rows_i = lt.shape[0] // (C_HI * C_LO)
    width = wh.shape[0] // (C_HI * C_LO)
    lanes = JB * width
    total_lanes = r_all.shape[1]
    chunk = min(total_lanes, 16 * lanes)
    steps = total_lanes // chunk
    nja_chunk = chunk // lanes
    out_rows = (total_lanes // lanes) * rows_i
    d = wh.shape[1]
    s = lt.shape[1]
    flops = 2 * lt.shape[0] * s * total_lanes + 3 * 2 * out_rows * (C_LO * lanes) * (JB * d) * C_HI
    return pl.pallas_call(
        functools.partial(outer_project_kernel, scale),
        grid=(steps,),
        in_specs=[
            pl.BlockSpec(lt.shape, lambda q: (0, 0)),
            pl.BlockSpec((s, chunk), lambda q: (0, q)),
            pl.BlockSpec(wh.shape, lambda q: (0, 0)),
            pl.BlockSpec(wl.shape, lambda q: (0, 0)),
        ],
        out_specs=pl.BlockSpec((nja_chunk * rows_i, JB * d), lambda q: (q, 0)),
        out_shape=jax.ShapeDtypeStruct((out_rows, JB * d), jnp.float32),
        scratch_shapes=[
            pltpu.VMEM((C_HI, C_LO * lanes, JB * d), jnp.bfloat16),
            pltpu.VMEM((C_HI, C_LO * lanes, JB * d), jnp.bfloat16),
        ],
        compiler_params=pltpu.CompilerParams(
            dimension_semantics=("arbitrary",), vmem_limit_bytes=48 * 1024 * 1024
        ),
        cost_estimate=pl.CostEstimate(
            flops=flops,
            transcendentals=0,
            bytes_accessed=lt.size * 2 + r_all.size * 2 + wh.size * 4 + out_rows * JB * d * 4,
        ),
    )(lt, r_all, wh, wl)


def norm_over_rows(values):
    mean = jnp.mean(values, axis=0, keepdims=True)
    centred = values - mean
    variance = jnp.mean(centred * centred, axis=0, keepdims=True)
    return centred * lax.rsqrt(variance + 1e-05)


def msa_kernel(x_ref, wwt_ref, wst_ref, pt_ref, o_ref, lt_ref, rt_ref):
    sites = x_ref.shape[0]
    width = pt_ref.shape[0] // 2
    wwt = wwt_ref[...]
    wst = wst_ref[...]
    pt = pt_ref[...]

    def body(i, carry):
        x = x_ref[i].astype(jnp.float32)
        n1 = norm_over_rows(x).astype(jnp.bfloat16)
        hidden = jnp.maximum(jnp.dot(wwt, n1, preferred_element_type=jnp.float32), 0.0).astype(jnp.bfloat16)
        refreshed = (x + jnp.dot(wst, hidden, preferred_element_type=jnp.float32)).astype(jnp.bfloat16)
        o_ref[i] = refreshed
        n2 = norm_over_rows(refreshed.astype(jnp.float32)).astype(jnp.bfloat16)
        proj = jnp.dot(pt, n2, preferred_element_type=jnp.float32)
        start = pl.multiple_of(i * width, width)
        lt_ref[pl.ds(start, width), :] = proj[:width]
        rt_ref[pl.ds(start, width), :] = proj[width:].astype(jnp.bfloat16)
        return carry

    lax.fori_loop(0, sites, body, 0, unroll=2)


def msa_block(xt, wwt, wst, pt):
    sites, k, depth = xt.shape
    width = pt.shape[0] // 2
    hidden = wwt.shape[0]
    return pl.pallas_call(
        msa_kernel,
        out_shape=(
            jax.ShapeDtypeStruct(xt.shape, jnp.bfloat16),
            jax.ShapeDtypeStruct((sites * width, depth), jnp.float32),
            jax.ShapeDtypeStruct((sites * width, depth), jnp.bfloat16),
        ),
        in_specs=[pl.BlockSpec(memory_space=pltpu.VMEM)] * 4,
        out_specs=(pl.BlockSpec(memory_space=pltpu.VMEM),) * 3,
        compiler_params=pltpu.CompilerParams(vmem_limit_bytes=32 * 1024 * 1024),
        cost_estimate=pl.CostEstimate(
            flops=2 * sites * depth * k * (2 * hidden + 2 * width),
            transcendentals=2 * sites * depth,
            bytes_accessed=sites * depth * (k * 4 + width * 6),
        ),
    )(xt, wwt, wst, pt)


def reduce_over_sequences(partial_value):
    nseq = lax.axis_size("seq")
    nchan = lax.axis_size("chan")
    if nchan != 2:
        return lax.psum_scatter(partial_value, ("seq", "chan"), scatter_dimension=0, tiled=True)
    rows, cols = partial_value.shape
    chunk = rows // (nseq * nchan)
    xs = partial_value.reshape(nseq, nchan, chunk, cols)
    c = lax.axis_index("chan")
    mine = lax.dynamic_index_in_dim(xs, c, axis=1, keepdims=False)
    other = lax.dynamic_index_in_dim(xs, 1 - c, axis=1, keepdims=False)
    received = lax.ppermute(other, "chan", [(0, 1), (1, 0)])
    part = mine + received
    if nseq > 4:
        gathered = lax.all_to_all(part, "seq", 0, 0, tiled=False)
        return gathered.sum(axis=0)
    me = lax.axis_index("seq")
    acc = lax.dynamic_index_in_dim(part, me, axis=0, keepdims=False)
    for k in range(1, nseq):
        src = lax.dynamic_index_in_dim(part, (me + k) % nseq, axis=0, keepdims=False)
        acc = acc + lax.ppermute(src, "seq", [(q, (q + k) % nseq) for q in range(nseq)])
    return acc


def per_device(
    homolog_embedding,
    coupling_embedding,
    homolog_widen_weights,
    homolog_shrink_weights,
    lhs_projector,
    rhs_projector,
    moment_coupling_weights,
    coupling_widen_weights,
    coupling_shrink_weights,
):
    homologs_local_share, sites_local_share, homolog_lane_number = homolog_embedding.shape
    proj_width = lhs_projector.shape[1]
    pair_width = coupling_embedding.shape[2]
    xt = jnp.transpose(homolog_embedding, (1, 2, 0))
    pt = jnp.concatenate([lhs_projector, rhs_projector], axis=1).T
    refreshed_t, left_t, right_t = msa_block(xt, homolog_widen_weights.T, homolog_shrink_weights.T, pt)
    homolog_refreshed = jnp.transpose(refreshed_t, (2, 0, 1))
    lt = (
        left_t.reshape(sites_local_share, proj_width, homologs_local_share)
        .transpose(1, 0, 2)
        .reshape(proj_width * sites_local_share, homologs_local_share)
    )
    right_features = right_t.T
    owners = lax.axis_size(("seq", "chan"))
    depth_total = float(homologs_local_share * owners)
    block_cols = coupling_embedding.shape[1]

    w_hi_f32 = lax.reduce_precision(moment_coupling_weights, exponent_bits=8, mantissa_bits=7)
    w_hi = w_hi_f32.astype(jnp.bfloat16)
    w_lo = (moment_coupling_weights - w_hi_f32).astype(jnp.bfloat16)
    nres = lax.axis_size("res")
    if nres == 2:
        r_other = lax.ppermute(right_features, "res", [(0, 1), (1, 0)])
        p_own = outer_project(lt, right_features, w_hi, w_lo, 1.0 / depth_total)
        p_other = outer_project(lt, r_other, w_hi, w_lo, 1.0 / depth_total)
        first = lax.axis_index("res") == 0
        partial_value = jnp.where(
            first, jnp.concatenate([p_own, p_other], axis=0), jnp.concatenate([p_other, p_own], axis=0)
        )
    else:
        r_all = lax.all_gather(right_features, "res", axis=1, tiled=True)
        partial_value = outer_project(lt, r_all, w_hi, w_lo, 1.0 / depth_total)
    pair_update = reduce_over_sequences(partial_value)
    nja_local = block_cols // JB
    pair_update = (
        pair_update.reshape(nja_local, sites_local_share, JB, pair_width)
        .transpose(1, 0, 2, 3)
        .reshape(sites_local_share * block_cols, pair_width)
    )
    pair_mid = coupling_embedding.reshape(sites_local_share * block_cols, pair_width) + pair_update
    pair_norm = apply_layer_norm(pair_mid).astype(jnp.bfloat16)
    pair_hidden = jnp.maximum(
        jnp.dot(pair_norm, coupling_widen_weights, preferred_element_type=jnp.float32), 0.0
    ).astype(jnp.bfloat16)
    coupling_refreshed = pair_mid + jnp.dot(
        pair_hidden, coupling_shrink_weights, preferred_element_type=jnp.float32
    )
    return (
        homolog_refreshed,
        coupling_refreshed.reshape(sites_local_share, block_cols, pair_width),
    )


def solution(mesh):
    return jax.shard_map(
        per_device,
        mesh=mesh,
        in_specs=(
            P(("groups", "seq", "chan"), "res", None),
            P(("groups", "res"), ("seq", "chan"), None),
            P(),
            P(),
            P(),
            P(),
            P(),
            P(),
            P(),
        ),
        out_specs=(
            P(("groups", "seq", "chan"), "res", None),
            P(("groups", "res"), ("seq", "chan"), None),
        ),
        check_vma=False,
    )
```

```python
import functools

import jax
import jax.numpy as jnp
from jax import lax
from jax.experimental import pallas as pl
from jax.experimental.pallas import tpu as pltpu
from jax.sharding import PartitionSpec as P


def apply_layer_norm(values):
    mean = jnp.mean(values, axis=-1, keepdims=True)
    centred = values - mean
    variance = jnp.mean(centred * centred, axis=-1, keepdims=True)
    return centred * lax.rsqrt(variance + 1e-05)


C_HI = 8
C_LO = 4
JB = 4


def outer_project_kernel(scale, lt_ref, r_ref, wh_ref, wl_ref, o_ref, vh_ref, vl_ref):
    width = wh_ref.shape[0] // (C_HI * C_LO)
    rows_i = lt_ref.shape[0] // (C_HI * C_LO)
    lanes = JB * width
    nja = r_ref.shape[1] // lanes
    dd = wh_ref.shape[1]

    @pl.when(pl.program_id(0) == 0)
    def _build():
        vh_ref[...] = jnp.zeros_like(vh_ref)
        vl_ref[...] = jnp.zeros_like(vl_ref)
        for c_hi in range(C_HI):
            for c_lo in range(C_LO):
                src = (c_hi * C_LO + c_lo) * width
                for jb in range(JB):
                    row = c_lo * lanes + jb * width
                    vh_ref[c_hi, row : row + width, jb * dd : (jb + 1) * dd] = wh_ref[src : src + width, :]
                    vl_ref[c_hi, row : row + width, jb * dd : (jb + 1) * dd] = wl_ref[src : src + width, :]

    def rearrange(y):
        return jnp.concatenate(
            [
                jnp.concatenate(
                    [y[c_lo * rows_i : (c_lo + 1) * rows_i, ja * lanes : (ja + 1) * lanes] for c_lo in range(C_LO)],
                    axis=1,
                )
                for ja in range(nja)
            ],
            axis=0,
        )

    acc = jnp.zeros(o_ref.shape, jnp.float32)
    block = C_LO * rows_i
    for c_hi in range(C_HI):
        x = jnp.dot(lt_ref[c_hi * block : (c_hi + 1) * block, :], r_ref[...], preferred_element_type=jnp.float32)
        xh = x.astype(jnp.bfloat16)
        xl = (x - xh.astype(jnp.float32)).astype(jnp.bfloat16)
        lh = rearrange(xh)
        ll = rearrange(xl)
        vh = vh_ref[c_hi]
        acc = acc + jnp.dot(lh, vh, preferred_element_type=jnp.float32)
        acc = acc + jnp.dot(ll, vh, preferred_element_type=jnp.float32)
        acc = acc + jnp.dot(lh, vl_ref[c_hi], preferred_element_type=jnp.float32)
    o_ref[...] = acc * scale


def outer_project(lt, r_all, wh, wl, scale):
    rows_i = lt.shape[0] // (C_HI * C_LO)
    width = wh.shape[0] // (C_HI * C_LO)
    lanes = JB * width
    total_lanes = r_all.shape[1]
    chunk = min(total_lanes, 16 * lanes)
    steps = total_lanes // chunk
    nja_chunk = chunk // lanes
    out_rows = (total_lanes // lanes) * rows_i
    d = wh.shape[1]
    s = lt.shape[1]
    flops = 2 * lt.shape[0] * s * total_lanes + 3 * 2 * out_rows * (C_LO * lanes) * (JB * d) * C_HI
    return pl.pallas_call(
        functools.partial(outer_project_kernel, scale),
        grid=(steps,),
        in_specs=[
            pl.BlockSpec(lt.shape, lambda q: (0, 0)),
            pl.BlockSpec((s, chunk), lambda q: (0, q)),
            pl.BlockSpec(wh.shape, lambda q: (0, 0)),
            pl.BlockSpec(wl.shape, lambda q: (0, 0)),
        ],
        out_specs=pl.BlockSpec((nja_chunk * rows_i, JB * d), lambda q: (q, 0)),
        out_shape=jax.ShapeDtypeStruct((out_rows, JB * d), jnp.float32),
        scratch_shapes=[
            pltpu.VMEM((C_HI, C_LO * lanes, JB * d), jnp.bfloat16),
            pltpu.VMEM((C_HI, C_LO * lanes, JB * d), jnp.bfloat16),
        ],
        compiler_params=pltpu.CompilerParams(
            dimension_semantics=("arbitrary",), vmem_limit_bytes=48 * 1024 * 1024
        ),
        cost_estimate=pl.CostEstimate(
            flops=flops,
            transcendentals=0,
            bytes_accessed=lt.size * 2 + r_all.size * 2 + wh.size * 4 + out_rows * JB * d * 4,
        ),
    )(lt, r_all, wh, wl)


def norm_over_rows(values):
    mean = jnp.mean(values, axis=0, keepdims=True)
    centred = values - mean
    variance = jnp.mean(centred * centred, axis=0, keepdims=True)
    return centred * lax.rsqrt(variance + 1e-05)


def msa_kernel(x_ref, wwt_ref, wst_ref, pt_ref, o_ref, lt_ref, rt_ref):
    sites = x_ref.shape[0]
    width = pt_ref.shape[0] // 2
    wwt = wwt_ref[...]
    wst = wst_ref[...]
    pt = pt_ref[...]

    def body(i, carry):
        x = x_ref[i].astype(jnp.float32)
        n1 = norm_over_rows(x).astype(jnp.bfloat16)
        hidden = jnp.maximum(jnp.dot(wwt, n1, preferred_element_type=jnp.float32), 0.0).astype(jnp.bfloat16)
        refreshed = (x + jnp.dot(wst, hidden, preferred_element_type=jnp.float32)).astype(jnp.bfloat16)
        o_ref[i] = refreshed
        n2 = norm_over_rows(refreshed.astype(jnp.float32)).astype(jnp.bfloat16)
        proj = jnp.dot(pt, n2, preferred_element_type=jnp.float32)
        start = pl.multiple_of(i * width, width)
        lt_ref[pl.ds(start, width), :] = proj[:width]
        rt_ref[pl.ds(start, width), :] = proj[width:].astype(jnp.bfloat16)
        return carry

    lax.fori_loop(0, sites, body, 0, unroll=True)


def msa_block(xt, wwt, wst, pt):
    sites, k, depth = xt.shape
    width = pt.shape[0] // 2
    hidden = wwt.shape[0]
    return pl.pallas_call(
        msa_kernel,
        out_shape=(
            jax.ShapeDtypeStruct(xt.shape, jnp.bfloat16),
            jax.ShapeDtypeStruct((sites * width, depth), jnp.float32),
            jax.ShapeDtypeStruct((sites * width, depth), jnp.bfloat16),
        ),
        in_specs=[pl.BlockSpec(memory_space=pltpu.VMEM)] * 4,
        out_specs=(pl.BlockSpec(memory_space=pltpu.VMEM),) * 3,
        compiler_params=pltpu.CompilerParams(vmem_limit_bytes=32 * 1024 * 1024),
        cost_estimate=pl.CostEstimate(
            flops=2 * sites * depth * k * (2 * hidden + 2 * width),
            transcendentals=2 * sites * depth,
            bytes_accessed=sites * depth * (k * 4 + width * 6),
        ),
    )(xt, wwt, wst, pt)


def reduce_over_sequences(partial_value):
    nseq = lax.axis_size("seq")
    nchan = lax.axis_size("chan")
    if nchan != 2:
        return lax.psum_scatter(partial_value, ("seq", "chan"), scatter_dimension=0, tiled=True)
    rows, cols = partial_value.shape
    chunk = rows // (nseq * nchan)
    xs = partial_value.reshape(nseq, nchan, chunk, cols)
    c = lax.axis_index("chan")
    mine = lax.dynamic_index_in_dim(xs, c, axis=1, keepdims=False)
    other = lax.dynamic_index_in_dim(xs, 1 - c, axis=1, keepdims=False)
    received = lax.ppermute(other, "chan", [(0, 1), (1, 0)])
    part = mine + received
    if nseq > 4:
        gathered = lax.all_to_all(part, "seq", 0, 0, tiled=False)
        return gathered.sum(axis=0)
    me = lax.axis_index("seq")
    acc = lax.dynamic_index_in_dim(part, me, axis=0, keepdims=False)
    for k in range(1, nseq):
        src = lax.dynamic_index_in_dim(part, (me + k) % nseq, axis=0, keepdims=False)
        acc = acc + lax.ppermute(src, "seq", [(q, (q + k) % nseq) for q in range(nseq)])
    return acc


def per_device(
    homolog_embedding,
    coupling_embedding,
    homolog_widen_weights,
    homolog_shrink_weights,
    lhs_projector,
    rhs_projector,
    moment_coupling_weights,
    coupling_widen_weights,
    coupling_shrink_weights,
):
    homologs_local_share, sites_local_share, homolog_lane_number = homolog_embedding.shape
    proj_width = lhs_projector.shape[1]
    pair_width = coupling_embedding.shape[2]
    xt = jnp.transpose(homolog_embedding, (1, 2, 0))
    pt = jnp.concatenate([lhs_projector, rhs_projector], axis=1).T
    refreshed_t, left_t, right_t = msa_block(xt, homolog_widen_weights.T, homolog_shrink_weights.T, pt)
    homolog_refreshed = jnp.transpose(refreshed_t, (2, 0, 1))
    lt = (
        left_t.reshape(sites_local_share, proj_width, homologs_local_share)
        .transpose(1, 0, 2)
        .reshape(proj_width * sites_local_share, homologs_local_share)
    )
    right_features = right_t.T
    owners = lax.axis_size(("seq", "chan"))
    depth_total = float(homologs_local_share * owners)
    block_cols = coupling_embedding.shape[1]

    w_hi_f32 = lax.reduce_precision(moment_coupling_weights, exponent_bits=8, mantissa_bits=7)
    w_hi = w_hi_f32.astype(jnp.bfloat16)
    w_lo = (moment_coupling_weights - w_hi_f32).astype(jnp.bfloat16)
    nres = lax.axis_size("res")
    if nres == 2:
        r_other = lax.ppermute(right_features, "res", [(0, 1), (1, 0)])
        p_own = outer_project(lt, right_features, w_hi, w_lo, 1.0 / depth_total)
        p_other = outer_project(lt, r_other, w_hi, w_lo, 1.0 / depth_total)
        first = lax.axis_index("res") == 0
        partial_value = jnp.where(
            first, jnp.concatenate([p_own, p_other], axis=0), jnp.concatenate([p_other, p_own], axis=0)
        )
    else:
        r_all = lax.all_gather(right_features, "res", axis=1, tiled=True)
        partial_value = outer_project(lt, r_all, w_hi, w_lo, 1.0 / depth_total)
    pair_update = reduce_over_sequences(partial_value)
    nja_local = block_cols // JB
    pair_update = (
        pair_update.reshape(nja_local, sites_local_share, JB, pair_width)
        .transpose(1, 0, 2, 3)
        .reshape(sites_local_share * block_cols, pair_width)
    )
    pair_mid = coupling_embedding.reshape(sites_local_share * block_cols, pair_width) + pair_update
    pair_norm = apply_layer_norm(pair_mid).astype(jnp.bfloat16)
    pair_hidden = jnp.maximum(
        jnp.dot(pair_norm, coupling_widen_weights, preferred_element_type=jnp.float32), 0.0
    ).astype(jnp.bfloat16)
    coupling_refreshed = pair_mid + jnp.dot(
        pair_hidden, coupling_shrink_weights, preferred_element_type=jnp.float32
    )
    return (
        homolog_refreshed,
        coupling_refreshed.reshape(sites_local_share, block_cols, pair_width),
    )


def solution(mesh):
    return jax.shard_map(
        per_device,
        mesh=mesh,
        in_specs=(
            P(("groups", "seq", "chan"), "res", None),
            P(("groups", "res"), ("seq", "chan"), None),
            P(),
            P(),
            P(),
            P(),
            P(),
            P(),
            P(),
        ),
        out_specs=(
            P(("groups", "seq", "chan"), "res", None),
            P(("groups", "res"), ("seq", "chan"), None),
        ),
        check_vma=False,
    )
```

```python
import functools

import jax
import jax.numpy as jnp
from jax import lax
from jax.experimental import pallas as pl
from jax.experimental.pallas import tpu as pltpu
from jax.sharding import PartitionSpec as P


def apply_layer_norm(values):
    mean = jnp.mean(values, axis=-1, keepdims=True)
    centred = values - mean
    variance = jnp.mean(centred * centred, axis=-1, keepdims=True)
    return centred * lax.rsqrt(variance + 1e-05)


def apply_layer_norm_axis1(values):
    mean = jnp.mean(values, axis=1, keepdims=True)
    centred = values - mean
    variance = jnp.mean(centred * centred, axis=1, keepdims=True)
    return centred * lax.rsqrt(variance + 1e-05)


C_HI = 8
C_LO = 4
JB = 4


def outer_project_kernel(scale, lt_ref, r_ref, wh_ref, wl_ref, o_ref, vh_ref, vl_ref):
    width = wh_ref.shape[0] // (C_HI * C_LO)
    rows_i = lt_ref.shape[0] // (C_HI * C_LO)
    lanes = JB * width
    nja = r_ref.shape[1] // lanes
    dd = wh_ref.shape[1]

    @pl.when(pl.program_id(0) == 0)
    def _build():
        vh_ref[...] = jnp.zeros_like(vh_ref)
        vl_ref[...] = jnp.zeros_like(vl_ref)
        for c_hi in range(C_HI):
            for c_lo in range(C_LO):
                src = (c_hi * C_LO + c_lo) * width
                for jb in range(JB):
                    row = c_lo * lanes + jb * width
                    vh_ref[c_hi, row : row + width, jb * dd : (jb + 1) * dd] = wh_ref[src : src + width, :]
                    vl_ref[c_hi, row : row + width, jb * dd : (jb + 1) * dd] = wl_ref[src : src + width, :]

    def rearrange(y):
        return jnp.concatenate(
            [
                jnp.concatenate(
                    [y[c_lo * rows_i : (c_lo + 1) * rows_i, ja * lanes : (ja + 1) * lanes] for c_lo in range(C_LO)],
                    axis=1,
                )
                for ja in range(nja)
            ],
            axis=0,
        )

    acc = jnp.zeros(o_ref.shape, jnp.float32)
    block = C_LO * rows_i
    for c_hi in range(C_HI):
        x = jnp.dot(lt_ref[c_hi * block : (c_hi + 1) * block, :], r_ref[...], preferred_element_type=jnp.float32)
        xh = x.astype(jnp.bfloat16)
        xl = (x - xh.astype(jnp.float32)).astype(jnp.bfloat16)
        lh = rearrange(xh)
        ll = rearrange(xl)
        vh = vh_ref[c_hi]
        acc = acc + jnp.dot(lh, vh, preferred_element_type=jnp.float32)
        acc = acc + jnp.dot(ll, vh, preferred_element_type=jnp.float32)
        acc = acc + jnp.dot(lh, vl_ref[c_hi], preferred_element_type=jnp.float32)
    o_ref[...] = acc * scale


def outer_project(lt, r_all, wh, wl, scale):
    rows_i = lt.shape[0] // (C_HI * C_LO)
    width = wh.shape[0] // (C_HI * C_LO)
    lanes = JB * width
    total_lanes = r_all.shape[1]
    chunk = min(total_lanes, 16 * lanes)
    steps = total_lanes // chunk
    nja_chunk = chunk // lanes
    out_rows = (total_lanes // lanes) * rows_i
    d = wh.shape[1]
    s = lt.shape[1]
    flops = 2 * lt.shape[0] * s * total_lanes + 3 * 2 * out_rows * (C_LO * lanes) * (JB * d) * C_HI
    return pl.pallas_call(
        functools.partial(outer_project_kernel, scale),
        grid=(steps,),
        in_specs=[
            pl.BlockSpec(lt.shape, lambda q: (0, 0)),
            pl.BlockSpec((s, chunk), lambda q: (0, q)),
            pl.BlockSpec(wh.shape, lambda q: (0, 0)),
            pl.BlockSpec(wl.shape, lambda q: (0, 0)),
        ],
        out_specs=pl.BlockSpec((nja_chunk * rows_i, JB * d), lambda q: (q, 0)),
        out_shape=jax.ShapeDtypeStruct((out_rows, JB * d), jnp.float32),
        scratch_shapes=[
            pltpu.VMEM((C_HI, C_LO * lanes, JB * d), jnp.bfloat16),
            pltpu.VMEM((C_HI, C_LO * lanes, JB * d), jnp.bfloat16),
        ],
        compiler_params=pltpu.CompilerParams(
            dimension_semantics=("arbitrary",), vmem_limit_bytes=48 * 1024 * 1024
        ),
        cost_estimate=pl.CostEstimate(
            flops=flops,
            transcendentals=0,
            bytes_accessed=lt.size * 2 + r_all.size * 2 + wh.size * 4 + out_rows * JB * d * 4,
        ),
    )(lt, r_all, wh, wl)


def reduce_over_sequences(partial_value):
    nseq = lax.axis_size("seq")
    nchan = lax.axis_size("chan")
    if nchan != 2:
        return lax.psum_scatter(partial_value, ("seq", "chan"), scatter_dimension=0, tiled=True)
    rows, cols = partial_value.shape
    chunk = rows // (nseq * nchan)
    xs = partial_value.reshape(nseq, nchan, chunk, cols)
    c = lax.axis_index("chan")
    mine = lax.dynamic_index_in_dim(xs, c, axis=1, keepdims=False)
    other = lax.dynamic_index_in_dim(xs, 1 - c, axis=1, keepdims=False)
    received = lax.ppermute(other, "chan", [(0, 1), (1, 0)])
    part = mine + received
    if nseq > 4:
        gathered = lax.all_to_all(part, "seq", 0, 0, tiled=False)
        return gathered.sum(axis=0)
    me = lax.axis_index("seq")
    acc = lax.dynamic_index_in_dim(part, me, axis=0, keepdims=False)
    for k in range(1, nseq):
        src = lax.dynamic_index_in_dim(part, (me + k) % nseq, axis=0, keepdims=False)
        acc = acc + lax.ppermute(src, "seq", [(q, (q + k) % nseq) for q in range(nseq)])
    return acc


def per_device(
    homolog_embedding,
    coupling_embedding,
    homolog_widen_weights,
    homolog_shrink_weights,
    lhs_projector,
    rhs_projector,
    moment_coupling_weights,
    coupling_widen_weights,
    coupling_shrink_weights,
):
    homologs_local_share, sites_local_share, homolog_lane_number = homolog_embedding.shape
    proj_width = lhs_projector.shape[1]
    pair_width = coupling_embedding.shape[2]
    xt = jnp.transpose(homolog_embedding, (1, 2, 0)).astype(jnp.float32)
    n1 = apply_layer_norm_axis1(xt).astype(jnp.bfloat16)
    hidden = jnp.maximum(
        jnp.einsum("kh,iks->ihs", homolog_widen_weights, n1, preferred_element_type=jnp.float32), 0.0
    ).astype(jnp.bfloat16)
    refreshed_t = (
        xt + jnp.einsum("hk,ihs->iks", homolog_shrink_weights, hidden, preferred_element_type=jnp.float32)
    ).astype(jnp.bfloat16)
    homolog_refreshed = jnp.transpose(refreshed_t, (2, 0, 1))
    n2 = apply_layer_norm_axis1(refreshed_t.astype(jnp.float32)).astype(jnp.bfloat16)
    lt = (
        jnp.einsum("kc,iks->cis", lhs_projector, n2, preferred_element_type=jnp.float32)
        .astype(jnp.bfloat16)
        .reshape(proj_width * sites_local_share, homologs_local_share)
    )
    right_features = (
        jnp.einsum("ke,iks->sie", rhs_projector, n2, preferred_element_type=jnp.float32)
        .astype(jnp.bfloat16)
        .reshape(homologs_local_share, sites_local_share * proj_width)
    )
    owners = lax.axis_size(("seq", "chan"))
    depth_total = float(homologs_local_share * owners)
    block_cols = coupling_embedding.shape[1]

    w_hi_f32 = lax.reduce_precision(moment_coupling_weights, exponent_bits=8, mantissa_bits=7)
    w_hi = w_hi_f32.astype(jnp.bfloat16)
    w_lo = (moment_coupling_weights - w_hi_f32).astype(jnp.bfloat16)
    nres = lax.axis_size("res")
    if nres == 2:
        r_other = lax.ppermute(right_features, "res", [(0, 1), (1, 0)])
        p_own = outer_project(lt, right_features, w_hi, w_lo, 1.0 / depth_total)
        p_other = outer_project(lt, r_other, w_hi, w_lo, 1.0 / depth_total)
        first = lax.axis_index("res") == 0
        partial_value = jnp.where(
            first, jnp.concatenate([p_own, p_other], axis=0), jnp.concatenate([p_other, p_own], axis=0)
        )
    else:
        r_all = lax.all_gather(right_features, "res", axis=1, tiled=True)
        partial_value = outer_project(lt, r_all, w_hi, w_lo, 1.0 / depth_total)
    pair_update = reduce_over_sequences(partial_value)
    nja_local = block_cols // JB
    pair_update = (
        pair_update.reshape(nja_local, sites_local_share, JB, pair_width)
        .transpose(1, 0, 2, 3)
        .reshape(sites_local_share * block_cols, pair_width)
    )
    pair_mid = coupling_embedding.reshape(sites_local_share * block_cols, pair_width) + pair_update
    pair_norm = apply_layer_norm(pair_mid).astype(jnp.bfloat16)
    pair_hidden = jnp.maximum(
        jnp.dot(pair_norm, coupling_widen_weights, preferred_element_type=jnp.float32), 0.0
    ).astype(jnp.bfloat16)
    coupling_refreshed = pair_mid + jnp.dot(
        pair_hidden, coupling_shrink_weights, preferred_element_type=jnp.float32
    )
    return (
        homolog_refreshed,
        coupling_refreshed.reshape(sites_local_share, block_cols, pair_width),
    )


def solution(mesh):
    return jax.shard_map(
        per_device,
        mesh=mesh,
        in_specs=(
            P(("groups", "seq", "chan"), "res", None),
            P(("groups", "res"), ("seq", "chan"), None),
            P(),
            P(),
            P(),
            P(),
            P(),
            P(),
            P(),
        ),
        out_specs=(
            P(("groups", "seq", "chan"), "res", None),
            P(("groups", "res"), ("seq", "chan"), None),
        ),
        check_vma=False,
    )
```

```python
import functools

import jax
import jax.numpy as jnp
from jax import lax
from jax.experimental import pallas as pl
from jax.experimental.pallas import tpu as pltpu
from jax.sharding import PartitionSpec as P


def apply_layer_norm(values):
    mean = jnp.mean(values, axis=-1, keepdims=True)
    centred = values - mean
    variance = jnp.mean(centred * centred, axis=-1, keepdims=True)
    return centred * lax.rsqrt(variance + 1e-05)


def apply_layer_norm_axis1(values):
    mean = jnp.mean(values, axis=1, keepdims=True)
    centred = values - mean
    variance = jnp.mean(centred * centred, axis=1, keepdims=True)
    return centred * lax.rsqrt(variance + 1e-05)


C_HI = 8
C_LO = 4
JB = 4


def outer_project_kernel(scale, lt_ref, r_ref, wh_ref, wl_ref, o_ref, vh_ref, vl_ref):
    width = wh_ref.shape[0] // (C_HI * C_LO)
    rows_i = lt_ref.shape[0] // (C_HI * C_LO)
    lanes = JB * width
    nja = r_ref.shape[1] // lanes
    dd = wh_ref.shape[1]

    @pl.when(pl.program_id(0) == 0)
    def _build():
        vh_ref[...] = jnp.zeros_like(vh_ref)
        vl_ref[...] = jnp.zeros_like(vl_ref)
        for c_hi in range(C_HI):
            for c_lo in range(C_LO):
                src = (c_hi * C_LO + c_lo) * width
                for jb in range(JB):
                    row = c_lo * lanes + jb * width
                    vh_ref[c_hi, row : row + width, jb * dd : (jb + 1) * dd] = wh_ref[src : src + width, :]
                    vl_ref[c_hi, row : row + width, jb * dd : (jb + 1) * dd] = wl_ref[src : src + width, :]

    def rearrange(y):
        return jnp.concatenate(
            [
                jnp.concatenate(
                    [y[c_lo * rows_i : (c_lo + 1) * rows_i, ja * lanes : (ja + 1) * lanes] for c_lo in range(C_LO)],
                    axis=1,
                )
                for ja in range(nja)
            ],
            axis=0,
        )

    acc = jnp.zeros(o_ref.shape, jnp.float32)
    block = C_LO * rows_i
    for c_hi in range(C_HI):
        x = jnp.dot(lt_ref[c_hi * block : (c_hi + 1) * block, :], r_ref[...], preferred_element_type=jnp.float32)
        xh = x.astype(jnp.bfloat16)
        xl = (x - xh.astype(jnp.float32)).astype(jnp.bfloat16)
        lh = rearrange(xh)
        ll = rearrange(xl)
        vh = vh_ref[c_hi]
        acc = acc + jnp.dot(lh, vh, preferred_element_type=jnp.float32)
        acc = acc + jnp.dot(ll, vh, preferred_element_type=jnp.float32)
        acc = acc + jnp.dot(lh, vl_ref[c_hi], preferred_element_type=jnp.float32)
    o_ref[...] = acc * scale


def outer_project(lt, r_all, wh, wl, scale):
    rows_i = lt.shape[0] // (C_HI * C_LO)
    width = wh.shape[0] // (C_HI * C_LO)
    lanes = JB * width
    total_lanes = r_all.shape[1]
    chunk = min(total_lanes, 16 * lanes)
    steps = total_lanes // chunk
    nja_chunk = chunk // lanes
    out_rows = (total_lanes // lanes) * rows_i
    d = wh.shape[1]
    s = lt.shape[1]
    flops = 2 * lt.shape[0] * s * total_lanes + 3 * 2 * out_rows * (C_LO * lanes) * (JB * d) * C_HI
    return pl.pallas_call(
        functools.partial(outer_project_kernel, scale),
        grid=(steps,),
        in_specs=[
            pl.BlockSpec(lt.shape, lambda q: (0, 0)),
            pl.BlockSpec((s, chunk), lambda q: (0, q)),
            pl.BlockSpec(wh.shape, lambda q: (0, 0)),
            pl.BlockSpec(wl.shape, lambda q: (0, 0)),
        ],
        out_specs=pl.BlockSpec((nja_chunk * rows_i, JB * d), lambda q: (q, 0)),
        out_shape=jax.ShapeDtypeStruct((out_rows, JB * d), jnp.float32),
        scratch_shapes=[
            pltpu.VMEM((C_HI, C_LO * lanes, JB * d), jnp.bfloat16),
            pltpu.VMEM((C_HI, C_LO * lanes, JB * d), jnp.bfloat16),
        ],
        compiler_params=pltpu.CompilerParams(
            dimension_semantics=("arbitrary",), vmem_limit_bytes=48 * 1024 * 1024
        ),
        cost_estimate=pl.CostEstimate(
            flops=flops,
            transcendentals=0,
            bytes_accessed=lt.size * 2 + r_all.size * 2 + wh.size * 4 + out_rows * JB * d * 4,
        ),
    )(lt, r_all, wh, wl)


def chan_stage(block, chunk):
    nchan = lax.axis_size("chan")
    rows, cols = block.shape
    xs = block.reshape(rows // (chunk * nchan), nchan, chunk, cols)
    c = lax.axis_index("chan")
    mine = lax.dynamic_index_in_dim(xs, c, axis=1, keepdims=False)
    other = lax.dynamic_index_in_dim(xs, 1 - c, axis=1, keepdims=False)
    return mine + lax.ppermute(other, "chan", [(0, 1), (1, 0)])


def seq_stage(part):
    nseq = lax.axis_size("seq")
    if nseq > 4:
        gathered = lax.all_to_all(part, "seq", 0, 0, tiled=False)
        return gathered.sum(axis=0)
    me = lax.axis_index("seq")
    acc = lax.dynamic_index_in_dim(part, me, axis=0, keepdims=False)
    for k in range(1, nseq):
        src = lax.dynamic_index_in_dim(part, (me + k) % nseq, axis=0, keepdims=False)
        acc = acc + lax.ppermute(src, "seq", [(q, (q + k) % nseq) for q in range(nseq)])
    return acc


def reduce_over_sequences(partial_value):
    if lax.axis_size("chan") != 2:
        return lax.psum_scatter(partial_value, ("seq", "chan"), scatter_dimension=0, tiled=True)
    chunk = partial_value.shape[0] // (lax.axis_size("seq") * lax.axis_size("chan"))
    return seq_stage(chan_stage(partial_value, chunk))


def per_device(
    homolog_embedding,
    coupling_embedding,
    homolog_widen_weights,
    homolog_shrink_weights,
    lhs_projector,
    rhs_projector,
    moment_coupling_weights,
    coupling_widen_weights,
    coupling_shrink_weights,
):
    homologs_local_share, sites_local_share, homolog_lane_number = homolog_embedding.shape
    proj_width = lhs_projector.shape[1]
    pair_width = coupling_embedding.shape[2]
    xt_all = jnp.transpose(homolog_embedding, (1, 2, 0))
    halves = 2 if sites_local_share % 16 == 0 else 1
    step = sites_local_share // halves
    refreshed_parts, lt_parts, right_parts = [], [], []
    for h in range(halves):
        xt = xt_all[h * step : (h + 1) * step].astype(jnp.float32)
        n1 = apply_layer_norm_axis1(xt).astype(jnp.bfloat16)
        hidden = jnp.maximum(
            jnp.einsum("kh,iks->ihs", homolog_widen_weights, n1, preferred_element_type=jnp.float32), 0.0
        ).astype(jnp.bfloat16)
        refreshed_t = (
            xt + jnp.einsum("hk,ihs->iks", homolog_shrink_weights, hidden, preferred_element_type=jnp.float32)
        ).astype(jnp.bfloat16)
        refreshed_parts.append(refreshed_t)
        n2 = apply_layer_norm_axis1(refreshed_t.astype(jnp.float32)).astype(jnp.bfloat16)
        right_parts.append(
            jnp.einsum("ke,iks->sie", rhs_projector, n2, preferred_element_type=jnp.float32)
            .astype(jnp.bfloat16)
            .reshape(homologs_local_share, step * proj_width)
        )
        lt_parts.append(
            jnp.einsum("kc,iks->cis", lhs_projector, n2, preferred_element_type=jnp.float32).astype(jnp.bfloat16)
        )
    homolog_refreshed = jnp.transpose(jnp.concatenate(refreshed_parts, axis=0), (2, 0, 1))
    lt = jnp.concatenate(lt_parts, axis=1).reshape(proj_width * sites_local_share, homologs_local_share)
    owners = lax.axis_size(("seq", "chan"))
    depth_total = float(homologs_local_share * owners)
    block_cols = coupling_embedding.shape[1]

    w_hi_f32 = lax.reduce_precision(moment_coupling_weights, exponent_bits=8, mantissa_bits=7)
    w_hi = w_hi_f32.astype(jnp.bfloat16)
    w_lo = (moment_coupling_weights - w_hi_f32).astype(jnp.bfloat16)
    nres = lax.axis_size("res")
    if nres == 2:
        r_other = jnp.concatenate([lax.ppermute(r, "res", [(0, 1), (1, 0)]) for r in right_parts], axis=1)
        r_own = jnp.concatenate(right_parts, axis=1)
        p_own = outer_project(lt, r_own, w_hi, w_lo, 1.0 / depth_total)
        chunk = 2 * p_own.shape[0] // (lax.axis_size("seq") * lax.axis_size("chan"))
        part_own = chan_stage(p_own, chunk)
        p_other = outer_project(lt, r_other, w_hi, w_lo, 1.0 / depth_total)
        part_other = chan_stage(p_other, chunk)
        first = lax.axis_index("res") == 0
        part = jnp.where(
            first, jnp.concatenate([part_own, part_other], axis=0), jnp.concatenate([part_other, part_own], axis=0)
        )
        pair_update = seq_stage(part)
    else:
        r_all = lax.all_gather(jnp.concatenate(right_parts, axis=1), "res", axis=1, tiled=True)
        partial_value = outer_project(lt, r_all, w_hi, w_lo, 1.0 / depth_total)
        pair_update = reduce_over_sequences(partial_value)
    nja_local = block_cols // JB
    pair_update = (
        pair_update.reshape(nja_local, sites_local_share, JB, pair_width)
        .transpose(1, 0, 2, 3)
        .reshape(sites_local_share * block_cols, pair_width)
    )
    pair_mid = coupling_embedding.reshape(sites_local_share * block_cols, pair_width) + pair_update
    pair_norm = apply_layer_norm(pair_mid).astype(jnp.bfloat16)
    pair_hidden = jnp.maximum(
        jnp.dot(pair_norm, coupling_widen_weights, preferred_element_type=jnp.float32), 0.0
    ).astype(jnp.bfloat16)
    coupling_refreshed = pair_mid + jnp.dot(
        pair_hidden, coupling_shrink_weights, preferred_element_type=jnp.float32
    )
    return (
        homolog_refreshed,
        coupling_refreshed.reshape(sites_local_share, block_cols, pair_width),
    )


def solution(mesh):
    return jax.shard_map(
        per_device,
        mesh=mesh,
        in_specs=(
            P(("groups", "seq", "chan"), "res", None),
            P(("groups", "res"), ("seq", "chan"), None),
            P(),
            P(),
            P(),
            P(),
            P(),
            P(),
            P(),
        ),
        out_specs=(
            P(("groups", "seq", "chan"), "res", None),
            P(("groups", "res"), ("seq", "chan"), None),
        ),
        check_vma=False,
    )
```

```python
import functools

import jax
import jax.numpy as jnp
from jax import lax
from jax.experimental import pallas as pl
from jax.experimental.pallas import tpu as pltpu
from jax.sharding import PartitionSpec as P


def apply_layer_norm(values):
    mean = jnp.mean(values, axis=-1, keepdims=True)
    centred = values - mean
    variance = jnp.mean(centred * centred, axis=-1, keepdims=True)
    return centred * lax.rsqrt(variance + 1e-05)


def apply_layer_norm_axis1(values):
    mean = jnp.mean(values, axis=1, keepdims=True)
    centred = values - mean
    variance = jnp.mean(centred * centred, axis=1, keepdims=True)
    return centred * lax.rsqrt(variance + 1e-05)


C_HI = 8
C_LO = 4
JB = 4


def outer_project_kernel(scale, build, lt_ref, r_ref, wh_ref, wl_ref, o_ref, vh_ref, vl_ref):
    width = wh_ref.shape[0] // (C_HI * C_LO)
    rows_i = lt_ref.shape[0] // (C_HI * C_LO)
    lanes = JB * width
    nja = r_ref.shape[1] // lanes
    dd = wh_ref.shape[1]

    if build:
        @pl.when(pl.program_id(0) == 0)
        def _build():
            vh_ref[...] = jnp.zeros_like(vh_ref)
            vl_ref[...] = jnp.zeros_like(vl_ref)
            for c_hi in range(C_HI):
                for c_lo in range(C_LO):
                    src = (c_hi * C_LO + c_lo) * width
                    for jb in range(JB):
                        row = c_lo * lanes + jb * width
                        vh_ref[c_hi, row : row + width, jb * dd : (jb + 1) * dd] = wh_ref[src : src + width, :]
                        vl_ref[c_hi, row : row + width, jb * dd : (jb + 1) * dd] = wl_ref[src : src + width, :]

    def rearrange(y):
        return jnp.concatenate(
            [
                jnp.concatenate(
                    [y[c_lo * rows_i : (c_lo + 1) * rows_i, ja * lanes : (ja + 1) * lanes] for c_lo in range(C_LO)],
                    axis=1,
                )
                for ja in range(nja)
            ],
            axis=0,
        )

    acc = jnp.zeros(o_ref.shape, jnp.float32)
    block = C_LO * rows_i
    for c_hi in range(C_HI):
        x = jnp.dot(lt_ref[c_hi * block : (c_hi + 1) * block, :], r_ref[...], preferred_element_type=jnp.float32)
        xh = x.astype(jnp.bfloat16)
        xl = (x - xh.astype(jnp.float32)).astype(jnp.bfloat16)
        lh = rearrange(xh)
        ll = rearrange(xl)
        vh = vh_ref[c_hi]
        acc = acc + jnp.dot(lh, vh, preferred_element_type=jnp.float32)
        acc = acc + jnp.dot(ll, vh, preferred_element_type=jnp.float32)
        acc = acc + jnp.dot(lh, vl_ref[c_hi], preferred_element_type=jnp.float32)
    o_ref[...] = acc * scale


def outer_project(lt, r_all, wh, wl, scale, weights=None):
    rows_i = lt.shape[0] // (C_HI * C_LO)
    width = wh.shape[0] // (C_HI * C_LO)
    lanes = JB * width
    total_lanes = r_all.shape[1]
    chunk = min(total_lanes, 16 * lanes)
    steps = total_lanes // chunk
    nja_chunk = chunk // lanes
    out_rows = (total_lanes // lanes) * rows_i
    d = wh.shape[1]
    s = lt.shape[1]
    flops = 2 * lt.shape[0] * s * total_lanes + 3 * 2 * out_rows * (C_LO * lanes) * (JB * d) * C_HI
    v_shape = jax.ShapeDtypeStruct((C_HI, C_LO * lanes, JB * d), jnp.bfloat16)
    vmem = pl.BlockSpec(memory_space=pltpu.VMEM)
    in_specs = [
        pl.BlockSpec(lt.shape, lambda q: (0, 0)),
        pl.BlockSpec((s, chunk), lambda q: (0, q)),
        pl.BlockSpec(wh.shape, lambda q: (0, 0)),
        pl.BlockSpec(wl.shape, lambda q: (0, 0)),
    ]
    out_block = pl.BlockSpec((nja_chunk * rows_i, JB * d), lambda q: (q, 0))
    out_shape = jax.ShapeDtypeStruct((out_rows, JB * d), jnp.float32)
    params = pltpu.CompilerParams(dimension_semantics=("arbitrary",), vmem_limit_bytes=48 * 1024 * 1024)
    cost = pl.CostEstimate(
        flops=flops,
        transcendentals=0,
        bytes_accessed=lt.size * 2 + r_all.size * 2 + wh.size * 4 + out_rows * JB * d * 4,
    )
    if weights is None:
        out, vh, vl = pl.pallas_call(
            functools.partial(outer_project_kernel, scale, True),
            grid=(steps,),
            in_specs=in_specs,
            out_specs=(out_block, vmem, vmem),
            out_shape=(out_shape, v_shape, v_shape),
            compiler_params=params,
            cost_estimate=cost,
        )(lt, r_all, wh, wl)
        return out, (vh, vl)

    def kernel(lt_ref, r_ref, wh_ref, wl_ref, vh_ref, vl_ref, o_ref):
        outer_project_kernel(scale, False, lt_ref, r_ref, wh_ref, wl_ref, o_ref, vh_ref, vl_ref)

    out = pl.pallas_call(
        kernel,
        grid=(steps,),
        in_specs=in_specs + [vmem, vmem],
        out_specs=out_block,
        out_shape=out_shape,
        compiler_params=params,
        cost_estimate=cost,
    )(lt, r_all, wh, wl, *weights)
    return out, weights

def chan_stage(block, chunk):
    nchan = lax.axis_size("chan")
    rows, cols = block.shape
    xs = block.reshape(rows // (chunk * nchan), nchan, chunk, cols)
    c = lax.axis_index("chan")
    mine = lax.dynamic_index_in_dim(xs, c, axis=1, keepdims=False)
    other = lax.dynamic_index_in_dim(xs, 1 - c, axis=1, keepdims=False)
    return mine + lax.ppermute(other, "chan", [(0, 1), (1, 0)])


def seq_stage(part):
    nseq = lax.axis_size("seq")
    if nseq > 4:
        gathered = lax.all_to_all(part, "seq", 0, 0, tiled=False)
        return gathered.sum(axis=0)
    me = lax.axis_index("seq")
    acc = lax.dynamic_index_in_dim(part, me, axis=0, keepdims=False)
    for k in range(1, nseq):
        src = lax.dynamic_index_in_dim(part, (me + k) % nseq, axis=0, keepdims=False)
        acc = acc + lax.ppermute(src, "seq", [(q, (q + k) % nseq) for q in range(nseq)])
    return acc


def reduce_over_sequences(partial_value):
    if lax.axis_size("chan") != 2:
        return lax.psum_scatter(partial_value, ("seq", "chan"), scatter_dimension=0, tiled=True)
    chunk = partial_value.shape[0] // (lax.axis_size("seq") * lax.axis_size("chan"))
    return seq_stage(chan_stage(partial_value, chunk))


def per_device(
    homolog_embedding,
    coupling_embedding,
    homolog_widen_weights,
    homolog_shrink_weights,
    lhs_projector,
    rhs_projector,
    moment_coupling_weights,
    coupling_widen_weights,
    coupling_shrink_weights,
):
    homologs_local_share, sites_local_share, homolog_lane_number = homolog_embedding.shape
    proj_width = lhs_projector.shape[1]
    pair_width = coupling_embedding.shape[2]
    xt_all = jnp.transpose(homolog_embedding, (1, 2, 0))
    halves = 2 if sites_local_share % 16 == 0 else 1
    step = sites_local_share // halves
    refreshed_parts, lt_parts, right_parts = [], [], []
    for h in range(halves):
        xt = xt_all[h * step : (h + 1) * step].astype(jnp.float32)
        n1 = apply_layer_norm_axis1(xt).astype(jnp.bfloat16)
        hidden = jnp.maximum(
            jnp.einsum("kh,iks->ihs", homolog_widen_weights, n1, preferred_element_type=jnp.float32), 0.0
        ).astype(jnp.bfloat16)
        refreshed_t = (
            xt + jnp.einsum("hk,ihs->iks", homolog_shrink_weights, hidden, preferred_element_type=jnp.float32)
        ).astype(jnp.bfloat16)
        refreshed_parts.append(refreshed_t)
        n2 = apply_layer_norm_axis1(refreshed_t.astype(jnp.float32)).astype(jnp.bfloat16)
        right_parts.append(
            jnp.einsum("ke,iks->sie", rhs_projector, n2, preferred_element_type=jnp.float32)
            .astype(jnp.bfloat16)
            .reshape(homologs_local_share, step * proj_width)
        )
        lt_parts.append(
            jnp.einsum("kc,iks->cis", lhs_projector, n2, preferred_element_type=jnp.float32).astype(jnp.bfloat16)
        )
    homolog_refreshed = jnp.transpose(jnp.concatenate(refreshed_parts, axis=0), (2, 0, 1))
    lt = jnp.concatenate(lt_parts, axis=1).reshape(proj_width * sites_local_share, homologs_local_share)
    owners = lax.axis_size(("seq", "chan"))
    depth_total = float(homologs_local_share * owners)
    block_cols = coupling_embedding.shape[1]

    w_hi_f32 = lax.reduce_precision(moment_coupling_weights, exponent_bits=8, mantissa_bits=7)
    w_hi = w_hi_f32.astype(jnp.bfloat16)
    w_lo = (moment_coupling_weights - w_hi_f32).astype(jnp.bfloat16)
    nres = lax.axis_size("res")
    if nres == 2:
        r_other = jnp.concatenate([lax.ppermute(r, "res", [(0, 1), (1, 0)]) for r in right_parts], axis=1)
        r_own = jnp.concatenate(right_parts, axis=1)
        p_own, weights = outer_project(lt, r_own, w_hi, w_lo, 1.0 / depth_total)
        chunk = 2 * p_own.shape[0] // (lax.axis_size("seq") * lax.axis_size("chan"))
        part_own = chan_stage(p_own, chunk)
        p_other, _ = outer_project(lt, r_other, w_hi, w_lo, 1.0 / depth_total, weights)
        part_other = chan_stage(p_other, chunk)
        first = lax.axis_index("res") == 0
        part = jnp.where(
            first, jnp.concatenate([part_own, part_other], axis=0), jnp.concatenate([part_other, part_own], axis=0)
        )
        pair_update = seq_stage(part)
    else:
        r_all = lax.all_gather(jnp.concatenate(right_parts, axis=1), "res", axis=1, tiled=True)
        partial_value, _ = outer_project(lt, r_all, w_hi, w_lo, 1.0 / depth_total)
        pair_update = reduce_over_sequences(partial_value)
    nja_local = block_cols // JB
    pair_update = (
        pair_update.reshape(nja_local, sites_local_share, JB, pair_width)
        .transpose(1, 0, 2, 3)
        .reshape(sites_local_share * block_cols, pair_width)
    )
    pair_mid = coupling_embedding.reshape(sites_local_share * block_cols, pair_width) + pair_update
    pair_norm = apply_layer_norm(pair_mid).astype(jnp.bfloat16)
    pair_hidden = jnp.maximum(
        jnp.dot(pair_norm, coupling_widen_weights, preferred_element_type=jnp.float32), 0.0
    ).astype(jnp.bfloat16)
    coupling_refreshed = pair_mid + jnp.dot(
        pair_hidden, coupling_shrink_weights, preferred_element_type=jnp.float32
    )
    return (
        homolog_refreshed,
        coupling_refreshed.reshape(sites_local_share, block_cols, pair_width),
    )


def solution(mesh):
    return jax.shard_map(
        per_device,
        mesh=mesh,
        in_specs=(
            P(("groups", "seq", "chan"), "res", None),
            P(("groups", "res"), ("seq", "chan"), None),
            P(),
            P(),
            P(),
            P(),
            P(),
            P(),
            P(),
        ),
        out_specs=(
            P(("groups", "seq", "chan"), "res", None),
            P(("groups", "res"), ("seq", "chan"), None),
        ),
        check_vma=False,
    )
```

```python
import functools

import jax
import jax.numpy as jnp
from jax import lax
from jax.experimental import pallas as pl
from jax.experimental.pallas import tpu as pltpu
from jax.sharding import PartitionSpec as P


def apply_layer_norm(values):
    mean = jnp.mean(values, axis=-1, keepdims=True)
    centred = values - mean
    variance = jnp.mean(centred * centred, axis=-1, keepdims=True)
    return centred * lax.rsqrt(variance + 1e-05)


def apply_layer_norm_axis1(values):
    mean = jnp.mean(values, axis=1, keepdims=True)
    centred = values - mean
    variance = jnp.mean(centred * centred, axis=1, keepdims=True)
    return centred * lax.rsqrt(variance + 1e-05)


C_HI = 8
C_LO = 4
JB = 4


def outer_project_kernel(scale, lt_ref, r_ref, wh_ref, wl_ref, o_ref, vh_ref, vl_ref):
    width = wh_ref.shape[0] // (C_HI * C_LO)
    rows_i = lt_ref.shape[0] // (C_HI * C_LO)
    lanes = JB * width
    nja = r_ref.shape[1] // lanes
    dd = wh_ref.shape[1]

    @pl.when(pl.program_id(0) == 0)
    def _build():
        vh_ref[...] = jnp.zeros_like(vh_ref)
        vl_ref[...] = jnp.zeros_like(vl_ref)
        for c_hi in range(C_HI):
            for c_lo in range(C_LO):
                src = (c_hi * C_LO + c_lo) * width
                for jb in range(JB):
                    row = c_lo * lanes + jb * width
                    vh_ref[c_hi, row : row + width, jb * dd : (jb + 1) * dd] = wh_ref[src : src + width, :]
                    vl_ref[c_hi, row : row + width, jb * dd : (jb + 1) * dd] = wl_ref[src : src + width, :]

    def rearrange(y):
        return jnp.concatenate(
            [
                jnp.concatenate(
                    [y[c_lo * rows_i : (c_lo + 1) * rows_i, ja * lanes : (ja + 1) * lanes] for c_lo in range(C_LO)],
                    axis=1,
                )
                for ja in range(nja)
            ],
            axis=0,
        )

    acc = jnp.zeros(o_ref.shape, jnp.float32)
    block = C_LO * rows_i
    for c_hi in range(C_HI):
        x = jnp.dot(lt_ref[c_hi * block : (c_hi + 1) * block, :], r_ref[...], preferred_element_type=jnp.float32)
        xh = x.astype(jnp.bfloat16)
        xl = (x - xh.astype(jnp.float32)).astype(jnp.bfloat16)
        lh = rearrange(xh)
        ll = rearrange(xl)
        vh = vh_ref[c_hi]
        acc = acc + jnp.dot(lh, vh, preferred_element_type=jnp.float32)
        acc = acc + jnp.dot(ll, vh, preferred_element_type=jnp.float32)
        acc = acc + jnp.dot(lh, vl_ref[c_hi], preferred_element_type=jnp.float32)
    o_ref[...] = acc * scale


def outer_project(lt, r_all, wh, wl, scale):
    rows_i = lt.shape[0] // (C_HI * C_LO)
    width = wh.shape[0] // (C_HI * C_LO)
    lanes = JB * width
    total_lanes = r_all.shape[1]
    chunk = min(total_lanes, 16 * lanes)
    steps = total_lanes // chunk
    nja_chunk = chunk // lanes
    out_rows = (total_lanes // lanes) * rows_i
    d = wh.shape[1]
    s = lt.shape[1]
    flops = 2 * lt.shape[0] * s * total_lanes + 3 * 2 * out_rows * (C_LO * lanes) * (JB * d) * C_HI
    return pl.pallas_call(
        functools.partial(outer_project_kernel, scale),
        grid=(steps,),
        in_specs=[
            pl.BlockSpec(lt.shape, lambda q: (0, 0)),
            pl.BlockSpec((s, chunk), lambda q: (0, q)),
            pl.BlockSpec(wh.shape, lambda q: (0, 0)),
            pl.BlockSpec(wl.shape, lambda q: (0, 0)),
        ],
        out_specs=pl.BlockSpec((nja_chunk * rows_i, JB * d), lambda q: (q, 0)),
        out_shape=jax.ShapeDtypeStruct((out_rows, JB * d), jnp.float32),
        scratch_shapes=[
            pltpu.VMEM((C_HI, C_LO * lanes, JB * d), jnp.bfloat16),
            pltpu.VMEM((C_HI, C_LO * lanes, JB * d), jnp.bfloat16),
        ],
        compiler_params=pltpu.CompilerParams(
            dimension_semantics=("arbitrary",), vmem_limit_bytes=48 * 1024 * 1024
        ),
        cost_estimate=pl.CostEstimate(
            flops=flops,
            transcendentals=0,
            bytes_accessed=lt.size * 2 + r_all.size * 2 + wh.size * 4 + out_rows * JB * d * 4,
        ),
    )(lt, r_all, wh, wl)


def pair_kernel(nj, u_ref, c_ref, ww_ref, ws_ref, o_ref):
    d = c_ref.shape[1]
    jbs = u_ref.shape[1] // d
    rows_i = c_ref.shape[0] // nj
    mids = []
    for j in range(nj):
        ja, jb = divmod(j, jbs)
        mids.append(
            c_ref[pl.ds(j, rows_i, stride=nj), :] + u_ref[ja * rows_i : (ja + 1) * rows_i, jb * d : (jb + 1) * d]
        )
    mid = jnp.concatenate(mids, axis=0)
    norm = apply_layer_norm(mid).astype(jnp.bfloat16)
    hidden = jnp.maximum(jnp.dot(norm, ww_ref[...], preferred_element_type=jnp.float32), 0.0).astype(jnp.bfloat16)
    out = mid + jnp.dot(hidden, ws_ref[...], preferred_element_type=jnp.float32)
    for j in range(nj):
        o_ref[pl.ds(j, rows_i, stride=nj), :] = out[j * rows_i : (j + 1) * rows_i]


def pair_transition(update, coupling, ww, ws, nj):
    rows, d = coupling.shape
    return pl.pallas_call(
        functools.partial(pair_kernel, nj),
        out_shape=jax.ShapeDtypeStruct((rows, d), jnp.float32),
        in_specs=[pl.BlockSpec(memory_space=pltpu.VMEM)] * 4,
        out_specs=pl.BlockSpec(memory_space=pltpu.VMEM),
        cost_estimate=pl.CostEstimate(
            flops=4 * rows * d * ww.shape[1], transcendentals=rows, bytes_accessed=rows * d * 12
        ),
    )(update, coupling, ww, ws)


def chan_stage(block, chunk):
    nchan = lax.axis_size("chan")
    rows, cols = block.shape
    xs = block.reshape(rows // (chunk * nchan), nchan, chunk, cols)
    c = lax.axis_index("chan")
    mine = lax.dynamic_index_in_dim(xs, c, axis=1, keepdims=False)
    other = lax.dynamic_index_in_dim(xs, 1 - c, axis=1, keepdims=False)
    return mine + lax.ppermute(other, "chan", [(0, 1), (1, 0)])


def seq_stage(part):
    nseq = lax.axis_size("seq")
    if nseq > 4:
        gathered = lax.all_to_all(part, "seq", 0, 0, tiled=False)
        return gathered.sum(axis=0)
    me = lax.axis_index("seq")
    acc = lax.dynamic_index_in_dim(part, me, axis=0, keepdims=False)
    for k in range(1, nseq):
        src = lax.dynamic_index_in_dim(part, (me + k) % nseq, axis=0, keepdims=False)
        acc = acc + lax.ppermute(src, "seq", [(q, (q + k) % nseq) for q in range(nseq)])
    return acc


def reduce_over_sequences(partial_value):
    if lax.axis_size("chan") != 2:
        return lax.psum_scatter(partial_value, ("seq", "chan"), scatter_dimension=0, tiled=True)
    chunk = partial_value.shape[0] // (lax.axis_size("seq") * lax.axis_size("chan"))
    return seq_stage(chan_stage(partial_value, chunk))


def per_device(
    homolog_embedding,
    coupling_embedding,
    homolog_widen_weights,
    homolog_shrink_weights,
    lhs_projector,
    rhs_projector,
    moment_coupling_weights,
    coupling_widen_weights,
    coupling_shrink_weights,
):
    homologs_local_share, sites_local_share, homolog_lane_number = homolog_embedding.shape
    proj_width = lhs_projector.shape[1]
    pair_width = coupling_embedding.shape[2]
    xt_all = jnp.transpose(homolog_embedding, (1, 2, 0))
    halves = 2 if sites_local_share % 16 == 0 else 1
    step = sites_local_share // halves
    refreshed_parts, lt_parts, right_parts = [], [], []
    for h in range(halves):
        xt = xt_all[h * step : (h + 1) * step].astype(jnp.float32)
        n1 = apply_layer_norm_axis1(xt).astype(jnp.bfloat16)
        hidden = jnp.maximum(
            jnp.einsum("kh,iks->ihs", homolog_widen_weights, n1, preferred_element_type=jnp.float32), 0.0
        ).astype(jnp.bfloat16)
        refreshed_t = (
            xt + jnp.einsum("hk,ihs->iks", homolog_shrink_weights, hidden, preferred_element_type=jnp.float32)
        ).astype(jnp.bfloat16)
        refreshed_parts.append(refreshed_t)
        n2 = apply_layer_norm_axis1(refreshed_t.astype(jnp.float32)).astype(jnp.bfloat16)
        right_parts.append(
            jnp.einsum("ke,iks->sie", rhs_projector, n2, preferred_element_type=jnp.float32)
            .astype(jnp.bfloat16)
            .reshape(homologs_local_share, step * proj_width)
        )
        lt_parts.append(
            jnp.einsum("kc,iks->cis", lhs_projector, n2, preferred_element_type=jnp.float32).astype(jnp.bfloat16)
        )
    homolog_refreshed = jnp.transpose(jnp.concatenate(refreshed_parts, axis=0), (2, 0, 1))
    lt = jnp.concatenate(lt_parts, axis=1).reshape(proj_width * sites_local_share, homologs_local_share)
    owners = lax.axis_size(("seq", "chan"))
    depth_total = float(homologs_local_share * owners)
    block_cols = coupling_embedding.shape[1]

    w_hi_f32 = lax.reduce_precision(moment_coupling_weights, exponent_bits=8, mantissa_bits=7)
    w_hi = w_hi_f32.astype(jnp.bfloat16)
    w_lo = (moment_coupling_weights - w_hi_f32).astype(jnp.bfloat16)
    nres = lax.axis_size("res")
    if nres == 2:
        r_other = jnp.concatenate([lax.ppermute(r, "res", [(0, 1), (1, 0)]) for r in right_parts], axis=1)
        r_own = jnp.concatenate(right_parts, axis=1)
        p_own = outer_project(lt, r_own, w_hi, w_lo, 1.0 / depth_total)
        chunk = 2 * p_own.shape[0] // (lax.axis_size("seq") * lax.axis_size("chan"))
        part_own = chan_stage(p_own, chunk)
        p_other = outer_project(lt, r_other, w_hi, w_lo, 1.0 / depth_total)
        part_other = chan_stage(p_other, chunk)
        first = lax.axis_index("res") == 0
        part = jnp.where(
            first, jnp.concatenate([part_own, part_other], axis=0), jnp.concatenate([part_other, part_own], axis=0)
        )
        pair_update = seq_stage(part)
    else:
        r_all = lax.all_gather(jnp.concatenate(right_parts, axis=1), "res", axis=1, tiled=True)
        partial_value = outer_project(lt, r_all, w_hi, w_lo, 1.0 / depth_total)
        pair_update = reduce_over_sequences(partial_value)
    coupling_refreshed = pair_transition(
        pair_update,
        coupling_embedding.reshape(sites_local_share * block_cols, pair_width),
        coupling_widen_weights,
        coupling_shrink_weights,
        block_cols,
    )
    return (
        homolog_refreshed,
        coupling_refreshed.reshape(sites_local_share, block_cols, pair_width),
    )


def solution(mesh):
    return jax.shard_map(
        per_device,
        mesh=mesh,
        in_specs=(
            P(("groups", "seq", "chan"), "res", None),
            P(("groups", "res"), ("seq", "chan"), None),
            P(),
            P(),
            P(),
            P(),
            P(),
            P(),
            P(),
        ),
        out_specs=(
            P(("groups", "seq", "chan"), "res", None),
            P(("groups", "res"), ("seq", "chan"), None),
        ),
        check_vma=False,
    )
```

```python
import functools

import jax
import jax.numpy as jnp
from jax import lax
from jax.experimental import pallas as pl
from jax.experimental.pallas import tpu as pltpu
from jax.sharding import PartitionSpec as P


def apply_layer_norm(values):
    mean = jnp.mean(values, axis=-1, keepdims=True)
    centred = values - mean
    variance = jnp.mean(centred * centred, axis=-1, keepdims=True)
    return centred * lax.rsqrt(variance + 1e-05)


def apply_layer_norm_axis1(values):
    mean = jnp.mean(values, axis=1, keepdims=True)
    centred = values - mean
    variance = jnp.mean(centred * centred, axis=1, keepdims=True)
    return centred * lax.rsqrt(variance + 1e-05)


C_HI = 8
C_LO = 4
JB = 4


def outer_project_kernel(scale, lt_ref, r_ref, wh_ref, wl_ref, o_ref, vh_ref, vl_ref):
    width = wh_ref.shape[0] // (C_HI * C_LO)
    rows_i = lt_ref.shape[0] // (C_HI * C_LO)
    lanes = JB * width
    nja = r_ref.shape[1] // lanes
    dd = wh_ref.shape[1]

    @pl.when(pl.program_id(0) == 0)
    def _build():
        vh_ref[...] = jnp.zeros_like(vh_ref)
        vl_ref[...] = jnp.zeros_like(vl_ref)
        for c_hi in range(C_HI):
            for c_lo in range(C_LO):
                src = (c_hi * C_LO + c_lo) * width
                for jb in range(JB):
                    row = c_lo * lanes + jb * width
                    vh_ref[c_hi, row : row + width, jb * dd : (jb + 1) * dd] = wh_ref[src : src + width, :]
                    vl_ref[c_hi, row : row + width, jb * dd : (jb + 1) * dd] = wl_ref[src : src + width, :]

    def rearrange(y):
        return jnp.concatenate(
            [
                jnp.concatenate(
                    [y[c_lo * rows_i : (c_lo + 1) * rows_i, ja * lanes : (ja + 1) * lanes] for c_lo in range(C_LO)],
                    axis=1,
                )
                for ja in range(nja)
            ],
            axis=0,
        )

    acc = jnp.zeros(o_ref.shape, jnp.float32)
    block = C_LO * rows_i
    for c_hi in range(C_HI):
        x = jnp.dot(lt_ref[c_hi * block : (c_hi + 1) * block, :], r_ref[...], preferred_element_type=jnp.float32)
        xh = x.astype(jnp.bfloat16)
        xl = (x - xh.astype(jnp.float32)).astype(jnp.bfloat16)
        lh = rearrange(xh)
        ll = rearrange(xl)
        vh = vh_ref[c_hi]
        acc = acc + jnp.dot(lh, vh, preferred_element_type=jnp.float32)
        acc = acc + jnp.dot(ll, vh, preferred_element_type=jnp.float32)
        acc = acc + jnp.dot(lh, vl_ref[c_hi], preferred_element_type=jnp.float32)
    o_ref[...] = acc * scale


def outer_project(lt, r_all, wh, wl, scale):
    rows_i = lt.shape[0] // (C_HI * C_LO)
    width = wh.shape[0] // (C_HI * C_LO)
    lanes = JB * width
    total_lanes = r_all.shape[1]
    chunk = min(total_lanes, 16 * lanes)
    steps = total_lanes // chunk
    nja_chunk = chunk // lanes
    out_rows = (total_lanes // lanes) * rows_i
    d = wh.shape[1]
    s = lt.shape[1]
    flops = 2 * lt.shape[0] * s * total_lanes + 3 * 2 * out_rows * (C_LO * lanes) * (JB * d) * C_HI
    return pl.pallas_call(
        functools.partial(outer_project_kernel, scale),
        grid=(steps,),
        in_specs=[
            pl.BlockSpec(lt.shape, lambda q: (0, 0)),
            pl.BlockSpec((s, chunk), lambda q: (0, q)),
            pl.BlockSpec(wh.shape, lambda q: (0, 0)),
            pl.BlockSpec(wl.shape, lambda q: (0, 0)),
        ],
        out_specs=pl.BlockSpec((nja_chunk * rows_i, JB * d), lambda q: (q, 0)),
        out_shape=jax.ShapeDtypeStruct((out_rows, JB * d), jnp.float32),
        scratch_shapes=[
            pltpu.VMEM((C_HI, C_LO * lanes, JB * d), jnp.bfloat16),
            pltpu.VMEM((C_HI, C_LO * lanes, JB * d), jnp.bfloat16),
        ],
        compiler_params=pltpu.CompilerParams(
            dimension_semantics=("arbitrary",), vmem_limit_bytes=48 * 1024 * 1024
        ),
        cost_estimate=pl.CostEstimate(
            flops=flops,
            transcendentals=0,
            bytes_accessed=lt.size * 2 + r_all.size * 2 + wh.size * 4 + out_rows * JB * d * 4,
        ),
    )(lt, r_all, wh, wl)


def chan_stage(block, chunk):
    nchan = lax.axis_size("chan")
    rows, cols = block.shape
    xs = block.reshape(rows // (chunk * nchan), nchan, chunk, cols)
    c = lax.axis_index("chan")
    mine = lax.dynamic_index_in_dim(xs, c, axis=1, keepdims=False)
    other = lax.dynamic_index_in_dim(xs, 1 - c, axis=1, keepdims=False)
    return mine + lax.ppermute(other, "chan", [(0, 1), (1, 0)])


def block_phase(part_blk, own_block):
    nseq = lax.axis_size("seq")
    half = nseq // 2
    me = lax.axis_index("seq")
    r = lax.axis_index("res")
    base_me = r * half if own_block else (1 - r) * half
    total = None
    for rho in range(1, nseq):
        pairs = []
        for a in range(nseq):
            for rr in range(2):
                d = (a + rho) % nseq
                base = rr * half if own_block else (1 - rr) * half
                if base <= d < base + half:
                    pairs.append((a * 2 + rr, d * 2 + rr))
        t = jnp.clip((me + rho) % nseq - base_me, 0, half - 1)
        src = lax.dynamic_index_in_dim(part_blk, t, axis=0, keepdims=False)
        got = lax.ppermute(src, ("seq", "res"), pairs)
        total = got if total is None else total + got
    return total


def seq_stage(part):
    nseq = lax.axis_size("seq")
    if nseq > 4:
        gathered = lax.all_to_all(part, "seq", 0, 0, tiled=False)
        return gathered.sum(axis=0)
    me = lax.axis_index("seq")
    acc = lax.dynamic_index_in_dim(part, me, axis=0, keepdims=False)
    for k in range(1, nseq):
        src = lax.dynamic_index_in_dim(part, (me + k) % nseq, axis=0, keepdims=False)
        acc = acc + lax.ppermute(src, "seq", [(q, (q + k) % nseq) for q in range(nseq)])
    return acc


def reduce_over_sequences(partial_value):
    if lax.axis_size("chan") != 2:
        return lax.psum_scatter(partial_value, ("seq", "chan"), scatter_dimension=0, tiled=True)
    chunk = partial_value.shape[0] // (lax.axis_size("seq") * lax.axis_size("chan"))
    return seq_stage(chan_stage(partial_value, chunk))


def per_device(
    homolog_embedding,
    coupling_embedding,
    homolog_widen_weights,
    homolog_shrink_weights,
    lhs_projector,
    rhs_projector,
    moment_coupling_weights,
    coupling_widen_weights,
    coupling_shrink_weights,
):
    homologs_local_share, sites_local_share, homolog_lane_number = homolog_embedding.shape
    proj_width = lhs_projector.shape[1]
    pair_width = coupling_embedding.shape[2]
    xt_all = jnp.transpose(homolog_embedding, (1, 2, 0))
    halves = 2 if sites_local_share % 16 == 0 else 1
    step = sites_local_share // halves
    refreshed_parts, lt_parts, right_parts = [], [], []
    for h in range(halves):
        xt = xt_all[h * step : (h + 1) * step].astype(jnp.float32)
        n1 = apply_layer_norm_axis1(xt).astype(jnp.bfloat16)
        hidden = jnp.maximum(
            jnp.einsum("kh,iks->ihs", homolog_widen_weights, n1, preferred_element_type=jnp.float32), 0.0
        ).astype(jnp.bfloat16)
        refreshed_t = (
            xt + jnp.einsum("hk,ihs->iks", homolog_shrink_weights, hidden, preferred_element_type=jnp.float32)
        ).astype(jnp.bfloat16)
        refreshed_parts.append(refreshed_t)
        n2 = apply_layer_norm_axis1(refreshed_t.astype(jnp.float32)).astype(jnp.bfloat16)
        right_parts.append(
            jnp.einsum("ke,iks->sie", rhs_projector, n2, preferred_element_type=jnp.float32)
            .astype(jnp.bfloat16)
            .reshape(homologs_local_share, step * proj_width)
        )
        lt_parts.append(
            jnp.einsum("kc,iks->cis", lhs_projector, n2, preferred_element_type=jnp.float32).astype(jnp.bfloat16)
        )
    homolog_refreshed = jnp.transpose(jnp.concatenate(refreshed_parts, axis=0), (2, 0, 1))
    lt = jnp.concatenate(lt_parts, axis=1).reshape(proj_width * sites_local_share, homologs_local_share)
    owners = lax.axis_size(("seq", "chan"))
    depth_total = float(homologs_local_share * owners)
    block_cols = coupling_embedding.shape[1]

    w_hi_f32 = lax.reduce_precision(moment_coupling_weights, exponent_bits=8, mantissa_bits=7)
    w_hi = w_hi_f32.astype(jnp.bfloat16)
    w_lo = (moment_coupling_weights - w_hi_f32).astype(jnp.bfloat16)
    nres = lax.axis_size("res")
    if nres == 2:
        r_other = jnp.concatenate([lax.ppermute(r, "res", [(0, 1), (1, 0)]) for r in right_parts], axis=1)
        r_own = jnp.concatenate(right_parts, axis=1)
        p_own = outer_project(lt, r_own, w_hi, w_lo, 1.0 / depth_total)
        chunk = 2 * p_own.shape[0] // (lax.axis_size("seq") * lax.axis_size("chan"))
        part_own = chan_stage(p_own, chunk)
        part_own, r_other = lax.optimization_barrier((part_own, r_other))
        received_own = block_phase(part_own, True)
        p_other = outer_project(lt, r_other, w_hi, w_lo, 1.0 / depth_total)
        received_own, p_other = lax.optimization_barrier((received_own, p_other))
        part_other = chan_stage(p_other, chunk)
        nseq = lax.axis_size("seq")
        half = nseq // 2
        me = lax.axis_index("seq")
        r = lax.axis_index("res")
        received_other = block_phase(part_other, False)
        kept_own = lax.dynamic_index_in_dim(part_own, jnp.clip(me - r * half, 0, half - 1), axis=0, keepdims=False)
        kept_other = lax.dynamic_index_in_dim(
            part_other, jnp.clip(me - (1 - r) * half, 0, half - 1), axis=0, keepdims=False
        )
        kept = jnp.where(me // half == r, kept_own, kept_other)
        pair_update = kept + received_own + received_other
    else:
        r_all = lax.all_gather(jnp.concatenate(right_parts, axis=1), "res", axis=1, tiled=True)
        partial_value = outer_project(lt, r_all, w_hi, w_lo, 1.0 / depth_total)
        pair_update = reduce_over_sequences(partial_value)
    nja_local = block_cols // JB
    pair_update = (
        pair_update.reshape(nja_local, sites_local_share, JB, pair_width)
        .transpose(1, 0, 2, 3)
        .reshape(sites_local_share * block_cols, pair_width)
    )
    pair_mid = coupling_embedding.reshape(sites_local_share * block_cols, pair_width) + pair_update
    pair_norm = apply_layer_norm(pair_mid).astype(jnp.bfloat16)
    pair_hidden = jnp.maximum(
        jnp.dot(pair_norm, coupling_widen_weights, preferred_element_type=jnp.float32), 0.0
    ).astype(jnp.bfloat16)
    coupling_refreshed = pair_mid + jnp.dot(
        pair_hidden, coupling_shrink_weights, preferred_element_type=jnp.float32
    )
    return (
        homolog_refreshed,
        coupling_refreshed.reshape(sites_local_share, block_cols, pair_width),
    )


def solution(mesh):
    return jax.shard_map(
        per_device,
        mesh=mesh,
        in_specs=(
            P(("groups", "seq", "chan"), "res", None),
            P(("groups", "res"), ("seq", "chan"), None),
            P(),
            P(),
            P(),
            P(),
            P(),
            P(),
            P(),
        ),
        out_specs=(
            P(("groups", "seq", "chan"), "res", None),
            P(("groups", "res"), ("seq", "chan"), None),
        ),
        check_vma=False,
    )
```

```python
import functools

import jax
import jax.numpy as jnp
from jax import lax
from jax.experimental import pallas as pl
from jax.experimental.pallas import tpu as pltpu
from jax.sharding import PartitionSpec as P


def apply_layer_norm(values):
    mean = jnp.mean(values, axis=-1, keepdims=True)
    centred = values - mean
    variance = jnp.mean(centred * centred, axis=-1, keepdims=True)
    return centred * lax.rsqrt(variance + 1e-05)


def apply_layer_norm_axis1(values):
    mean = jnp.mean(values, axis=1, keepdims=True)
    centred = values - mean
    variance = jnp.mean(centred * centred, axis=1, keepdims=True)
    return centred * lax.rsqrt(variance + 1e-05)


C_HI = 8
C_LO = 4
JB = 4


def outer_project_kernel(scale, nparts, *refs):
    lt_ref = refs[0]
    r_refs = refs[1 : 1 + nparts]
    wh_ref, wl_ref, o_ref, vh_ref, vl_ref = refs[1 + nparts :]
    width = wh_ref.shape[0] // (C_HI * C_LO)
    rows_i = lt_ref.shape[0] // (C_HI * C_LO)
    lanes = JB * width
    nja = sum(r.shape[1] for r in r_refs) // lanes
    dd = wh_ref.shape[1]

    @pl.when(pl.program_id(0) == 0)
    def _build():
        vh_ref[...] = jnp.zeros_like(vh_ref)
        vl_ref[...] = jnp.zeros_like(vl_ref)
        for c_hi in range(C_HI):
            for c_lo in range(C_LO):
                src = (c_hi * C_LO + c_lo) * width
                for jb in range(JB):
                    row = c_lo * lanes + jb * width
                    vh_ref[c_hi, row : row + width, jb * dd : (jb + 1) * dd] = wh_ref[src : src + width, :]
                    vl_ref[c_hi, row : row + width, jb * dd : (jb + 1) * dd] = wl_ref[src : src + width, :]

    def rearrange(y):
        return jnp.concatenate(
            [
                jnp.concatenate(
                    [y[c_lo * rows_i : (c_lo + 1) * rows_i, ja * lanes : (ja + 1) * lanes] for c_lo in range(C_LO)],
                    axis=1,
                )
                for ja in range(nja)
            ],
            axis=0,
        )

    acc = jnp.zeros(o_ref.shape, jnp.float32)
    block = C_LO * rows_i
    for c_hi in range(C_HI):
        lt_blk = lt_ref[c_hi * block : (c_hi + 1) * block, :]
        xs = [jnp.dot(lt_blk, r[...], preferred_element_type=jnp.float32) for r in r_refs]
        x = xs[0] if nparts == 1 else jnp.concatenate(xs, axis=1)
        xh = x.astype(jnp.bfloat16)
        xl = (x - xh.astype(jnp.float32)).astype(jnp.bfloat16)
        lh = rearrange(xh)
        ll = rearrange(xl)
        vh = vh_ref[c_hi]
        acc = acc + jnp.dot(lh, vh, preferred_element_type=jnp.float32)
        acc = acc + jnp.dot(ll, vh, preferred_element_type=jnp.float32)
        acc = acc + jnp.dot(lh, vl_ref[c_hi], preferred_element_type=jnp.float32)
    o_ref[...] = acc * scale


def outer_project(lt, r_parts, wh, wl, scale):
    nparts = len(r_parts)
    r_all = r_parts[0]
    rows_i = lt.shape[0] // (C_HI * C_LO)
    width = wh.shape[0] // (C_HI * C_LO)
    lanes = JB * width
    total_lanes = sum(r.shape[1] for r in r_parts)
    chunk = min(total_lanes, 16 * lanes)
    if nparts > 1:
        assert chunk == total_lanes
    steps = total_lanes // chunk
    nja_chunk = chunk // lanes
    out_rows = (total_lanes // lanes) * rows_i
    d = wh.shape[1]
    s = lt.shape[1]
    flops = 2 * lt.shape[0] * s * total_lanes + 3 * 2 * out_rows * (C_LO * lanes) * (JB * d) * C_HI
    return pl.pallas_call(
        functools.partial(outer_project_kernel, scale, nparts),
        grid=(steps,),
        in_specs=[
            pl.BlockSpec(lt.shape, lambda q: (0, 0)),
            *(
                [pl.BlockSpec((s, chunk), lambda q: (0, q))]
                if nparts == 1
                else [pl.BlockSpec(r.shape, lambda q: (0, 0)) for r in r_parts]
            ),
            pl.BlockSpec(wh.shape, lambda q: (0, 0)),
            pl.BlockSpec(wl.shape, lambda q: (0, 0)),
        ],
        out_specs=pl.BlockSpec((nja_chunk * rows_i, JB * d), lambda q: (q, 0)),
        out_shape=jax.ShapeDtypeStruct((out_rows, JB * d), jnp.float32),
        scratch_shapes=[
            pltpu.VMEM((C_HI, C_LO * lanes, JB * d), jnp.bfloat16),
            pltpu.VMEM((C_HI, C_LO * lanes, JB * d), jnp.bfloat16),
        ],
        compiler_params=pltpu.CompilerParams(
            dimension_semantics=("arbitrary",), vmem_limit_bytes=48 * 1024 * 1024
        ),
        cost_estimate=pl.CostEstimate(
            flops=flops,
            transcendentals=0,
            bytes_accessed=lt.size * 2 + total_lanes * s * 2 + wh.size * 4 + out_rows * JB * d * 4,
        ),
    )(lt, *r_parts, wh, wl)


def chan_stage(block, chunk):
    nchan = lax.axis_size("chan")
    rows, cols = block.shape
    xs = block.reshape(rows // (chunk * nchan), nchan, chunk, cols)
    c = lax.axis_index("chan")
    mine = lax.dynamic_index_in_dim(xs, c, axis=1, keepdims=False)
    other = lax.dynamic_index_in_dim(xs, 1 - c, axis=1, keepdims=False)
    return mine + lax.ppermute(other, "chan", [(0, 1), (1, 0)])


def seq_stage(part):
    nseq = lax.axis_size("seq")
    if nseq > 4:
        gathered = lax.all_to_all(part, "seq", 0, 0, tiled=False)
        return gathered.sum(axis=0)
    me = lax.axis_index("seq")
    acc = lax.dynamic_index_in_dim(part, me, axis=0, keepdims=False)
    for k in range(1, nseq):
        src = lax.dynamic_index_in_dim(part, (me + k) % nseq, axis=0, keepdims=False)
        acc = acc + lax.ppermute(src, "seq", [(q, (q + k) % nseq) for q in range(nseq)])
    return acc


def reduce_over_sequences(partial_value):
    if lax.axis_size("chan") != 2:
        return lax.psum_scatter(partial_value, ("seq", "chan"), scatter_dimension=0, tiled=True)
    chunk = partial_value.shape[0] // (lax.axis_size("seq") * lax.axis_size("chan"))
    return seq_stage(chan_stage(partial_value, chunk))


def per_device(
    homolog_embedding,
    coupling_embedding,
    homolog_widen_weights,
    homolog_shrink_weights,
    lhs_projector,
    rhs_projector,
    moment_coupling_weights,
    coupling_widen_weights,
    coupling_shrink_weights,
):
    homologs_local_share, sites_local_share, homolog_lane_number = homolog_embedding.shape
    proj_width = lhs_projector.shape[1]
    pair_width = coupling_embedding.shape[2]
    xt_all = jnp.transpose(homolog_embedding, (1, 2, 0))
    halves = 2 if sites_local_share % 16 == 0 else 1
    step = sites_local_share // halves
    refreshed_parts, lt_parts, right_parts = [], [], []
    for h in range(halves):
        xt = xt_all[h * step : (h + 1) * step].astype(jnp.float32)
        n1 = apply_layer_norm_axis1(xt).astype(jnp.bfloat16)
        hidden = jnp.maximum(
            jnp.einsum("kh,iks->ihs", homolog_widen_weights, n1, preferred_element_type=jnp.float32), 0.0
        ).astype(jnp.bfloat16)
        refreshed_t = (
            xt + jnp.einsum("hk,ihs->iks", homolog_shrink_weights, hidden, preferred_element_type=jnp.float32)
        ).astype(jnp.bfloat16)
        refreshed_parts.append(refreshed_t)
        n2 = apply_layer_norm_axis1(refreshed_t.astype(jnp.float32)).astype(jnp.bfloat16)
        right_parts.append(
            jnp.einsum("ke,iks->sie", rhs_projector, n2, preferred_element_type=jnp.float32)
            .astype(jnp.bfloat16)
            .reshape(homologs_local_share, step * proj_width)
        )
        lt_parts.append(
            jnp.einsum("kc,iks->cis", lhs_projector, n2, preferred_element_type=jnp.float32).astype(jnp.bfloat16)
        )
    homolog_refreshed = jnp.transpose(jnp.concatenate(refreshed_parts, axis=0), (2, 0, 1))
    lt = jnp.concatenate(lt_parts, axis=1).reshape(proj_width * sites_local_share, homologs_local_share)
    owners = lax.axis_size(("seq", "chan"))
    depth_total = float(homologs_local_share * owners)
    block_cols = coupling_embedding.shape[1]

    w_hi_f32 = lax.reduce_precision(moment_coupling_weights, exponent_bits=8, mantissa_bits=7)
    w_hi = w_hi_f32.astype(jnp.bfloat16)
    w_lo = (moment_coupling_weights - w_hi_f32).astype(jnp.bfloat16)
    nres = lax.axis_size("res")
    if nres == 2:
        r_other = [lax.ppermute(r, "res", [(0, 1), (1, 0)]) for r in right_parts]
        p_own = outer_project(lt, right_parts, w_hi, w_lo, 1.0 / depth_total)
        chunk = 2 * p_own.shape[0] // (lax.axis_size("seq") * lax.axis_size("chan"))
        part_own = chan_stage(p_own, chunk)
        p_other = outer_project(lt, r_other, w_hi, w_lo, 1.0 / depth_total)
        part_other = chan_stage(p_other, chunk)
        first = lax.axis_index("res") == 0
        part = jnp.where(
            first, jnp.concatenate([part_own, part_other], axis=0), jnp.concatenate([part_other, part_own], axis=0)
        )
        pair_update = seq_stage(part)
    else:
        r_all = lax.all_gather(jnp.concatenate(right_parts, axis=1), "res", axis=1, tiled=True)
        partial_value = outer_project(lt, [r_all], w_hi, w_lo, 1.0 / depth_total)
        pair_update = reduce_over_sequences(partial_value)
    nja_local = block_cols // JB
    pair_update = (
        pair_update.reshape(nja_local, sites_local_share, JB, pair_width)
        .transpose(1, 0, 2, 3)
        .reshape(sites_local_share * block_cols, pair_width)
    )
    pair_mid = coupling_embedding.reshape(sites_local_share * block_cols, pair_width) + pair_update
    pair_norm = apply_layer_norm(pair_mid).astype(jnp.bfloat16)
    pair_hidden = jnp.maximum(
        jnp.dot(pair_norm, coupling_widen_weights, preferred_element_type=jnp.float32), 0.0
    ).astype(jnp.bfloat16)
    coupling_refreshed = pair_mid + jnp.dot(
        pair_hidden, coupling_shrink_weights, preferred_element_type=jnp.float32
    )
    return (
        homolog_refreshed,
        coupling_refreshed.reshape(sites_local_share, block_cols, pair_width),
    )


def solution(mesh):
    return jax.shard_map(
        per_device,
        mesh=mesh,
        in_specs=(
            P(("groups", "seq", "chan"), "res", None),
            P(("groups", "res"), ("seq", "chan"), None),
            P(),
            P(),
            P(),
            P(),
            P(),
            P(),
            P(),
        ),
        out_specs=(
            P(("groups", "seq", "chan"), "res", None),
            P(("groups", "res"), ("seq", "chan"), None),
        ),
        check_vma=False,
    )
```

```python
import functools

import jax
import jax.numpy as jnp
from jax import lax
from jax.experimental import pallas as pl
from jax.experimental.pallas import tpu as pltpu
from jax.sharding import PartitionSpec as P


def apply_layer_norm(values):
    mean = jnp.mean(values, axis=-1, keepdims=True)
    centred = values - mean
    variance = jnp.mean(centred * centred, axis=-1, keepdims=True)
    return centred * lax.rsqrt(variance + 1e-05)


def apply_layer_norm_axis1(values):
    mean = jnp.mean(values, axis=1, keepdims=True)
    centred = values - mean
    variance = jnp.mean(centred * centred, axis=1, keepdims=True)
    return centred * lax.rsqrt(variance + 1e-05)


C_HI = 8
C_LO = 4
JB = 4


def outer_project_kernel(scale, nparts, *refs):
    lt_ref = refs[0]
    r_refs = refs[1 : 1 + nparts]
    wh_ref, wl_ref, o_ref, vh_ref, vl_ref = refs[1 + nparts :]
    width = wh_ref.shape[0] // (C_HI * C_LO)
    rows_i = lt_ref.shape[0] // (C_HI * C_LO)
    lanes = JB * width
    nja = sum(r.shape[1] for r in r_refs) // lanes
    dd = wh_ref.shape[1]

    @pl.when(pl.program_id(0) == 0)
    def _build():
        vh_ref[...] = jnp.zeros_like(vh_ref)
        vl_ref[...] = jnp.zeros_like(vl_ref)
        for c_hi in range(C_HI):
            for c_lo in range(C_LO):
                src = (c_hi * C_LO + c_lo) * width
                for jb in range(JB):
                    row = c_lo * lanes + jb * width
                    vh_ref[c_hi, row : row + width, jb * dd : (jb + 1) * dd] = wh_ref[src : src + width, :]
                    vl_ref[c_hi, row : row + width, jb * dd : (jb + 1) * dd] = wl_ref[src : src + width, :]

    def rearrange(y):
        return jnp.concatenate(
            [
                jnp.concatenate(
                    [y[c_lo * rows_i : (c_lo + 1) * rows_i, ja * lanes : (ja + 1) * lanes] for c_lo in range(C_LO)],
                    axis=1,
                )
                for ja in range(nja)
            ],
            axis=0,
        )

    acc = jnp.zeros(o_ref.shape, jnp.float32)
    block = C_LO * rows_i
    for c_hi in range(C_HI):
        lt_blk = lt_ref[c_hi * block : (c_hi + 1) * block, :]
        xs = [jnp.dot(lt_blk, r[...], preferred_element_type=jnp.float32) for r in r_refs]
        x = xs[0] if nparts == 1 else jnp.concatenate(xs, axis=1)
        xh = x.astype(jnp.bfloat16)
        xl = (x - xh.astype(jnp.float32)).astype(jnp.bfloat16)
        lh = rearrange(xh)
        ll = rearrange(xl)
        vh = vh_ref[c_hi]
        acc = acc + jnp.dot(lh, vh, preferred_element_type=jnp.float32)
        acc = acc + jnp.dot(ll, vh, preferred_element_type=jnp.float32)
        acc = acc + jnp.dot(lh, vl_ref[c_hi], preferred_element_type=jnp.float32)
    o_ref[...] = acc * scale


def outer_project(lt, r_parts, wh, wl, scale):
    nparts = len(r_parts)
    r_all = r_parts[0]
    rows_i = lt.shape[0] // (C_HI * C_LO)
    width = wh.shape[0] // (C_HI * C_LO)
    lanes = JB * width
    total_lanes = sum(r.shape[1] for r in r_parts)
    chunk = min(total_lanes, 16 * lanes)
    if nparts > 1:
        assert chunk == total_lanes
    steps = total_lanes // chunk
    nja_chunk = chunk // lanes
    out_rows = (total_lanes // lanes) * rows_i
    d = wh.shape[1]
    s = lt.shape[1]
    flops = 2 * lt.shape[0] * s * total_lanes + 3 * 2 * out_rows * (C_LO * lanes) * (JB * d) * C_HI
    return pl.pallas_call(
        functools.partial(outer_project_kernel, scale, nparts),
        grid=(steps,),
        in_specs=[
            pl.BlockSpec(lt.shape, lambda q: (0, 0)),
            *(
                [pl.BlockSpec((s, chunk), lambda q: (0, q))]
                if nparts == 1
                else [pl.BlockSpec(r.shape, lambda q: (0, 0)) for r in r_parts]
            ),
            pl.BlockSpec(wh.shape, lambda q: (0, 0)),
            pl.BlockSpec(wl.shape, lambda q: (0, 0)),
        ],
        out_specs=pl.BlockSpec((nja_chunk * rows_i, JB * d), lambda q: (q, 0)),
        out_shape=jax.ShapeDtypeStruct((out_rows, JB * d), jnp.float32),
        scratch_shapes=[
            pltpu.VMEM((C_HI, C_LO * lanes, JB * d), jnp.bfloat16),
            pltpu.VMEM((C_HI, C_LO * lanes, JB * d), jnp.bfloat16),
        ],
        compiler_params=pltpu.CompilerParams(
            dimension_semantics=("arbitrary",), vmem_limit_bytes=48 * 1024 * 1024
        ),
        cost_estimate=pl.CostEstimate(
            flops=flops,
            transcendentals=0,
            bytes_accessed=lt.size * 2 + total_lanes * s * 2 + wh.size * 4 + out_rows * JB * d * 4,
        ),
    )(lt, *r_parts, wh, wl)


def chan_stage(block, chunk):
    nchan = lax.axis_size("chan")
    rows, cols = block.shape
    xs = block.reshape(rows // (chunk * nchan), nchan, chunk, cols)
    first = lax.axis_index("chan") == 0
    mine = jnp.where(first, xs[:, 0], xs[:, 1])
    other = jnp.where(first, xs[:, 1], xs[:, 0])
    return mine + lax.ppermute(other, "chan", [(0, 1), (1, 0)])


def seq_stage(part):
    nseq = lax.axis_size("seq")
    if nseq > 4:
        gathered = lax.all_to_all(part, "seq", 0, 0, tiled=False)
        return gathered.sum(axis=0)
    me = lax.axis_index("seq")
    acc = lax.dynamic_index_in_dim(part, me, axis=0, keepdims=False)
    for k in range(1, nseq):
        src = lax.dynamic_index_in_dim(part, (me + k) % nseq, axis=0, keepdims=False)
        acc = acc + lax.ppermute(src, "seq", [(q, (q + k) % nseq) for q in range(nseq)])
    return acc


def seq_stage_blocks(part_own, part_other):
    nseq = lax.axis_size("seq")
    half = part_own.shape[0]
    me = lax.axis_index("seq")
    r = lax.axis_index("res")

    def entry(t):
        q = t % half
        own = lax.dynamic_index_in_dim(part_own, q, axis=0, keepdims=False)
        other = lax.dynamic_index_in_dim(part_other, q, axis=0, keepdims=False)
        return jnp.where(t // half == r, own, other)

    acc = entry(me)
    for k in range(1, nseq):
        src = entry((me + k) % nseq)
        acc = acc + lax.ppermute(src, "seq", [(q, (q + k) % nseq) for q in range(nseq)])
    return acc


def reduce_over_sequences(partial_value):
    if lax.axis_size("chan") != 2:
        return lax.psum_scatter(partial_value, ("seq", "chan"), scatter_dimension=0, tiled=True)
    chunk = partial_value.shape[0] // (lax.axis_size("seq") * lax.axis_size("chan"))
    return seq_stage(chan_stage(partial_value, chunk))


def per_device(
    homolog_embedding,
    coupling_embedding,
    homolog_widen_weights,
    homolog_shrink_weights,
    lhs_projector,
    rhs_projector,
    moment_coupling_weights,
    coupling_widen_weights,
    coupling_shrink_weights,
):
    homologs_local_share, sites_local_share, homolog_lane_number = homolog_embedding.shape
    proj_width = lhs_projector.shape[1]
    pair_width = coupling_embedding.shape[2]
    xt_all = jnp.transpose(homolog_embedding, (1, 2, 0))
    halves = 2 if sites_local_share % 16 == 0 else 1
    step = sites_local_share // halves
    refreshed_parts, lt_parts, right_parts = [], [], []
    for h in range(halves):
        xt = xt_all[h * step : (h + 1) * step].astype(jnp.float32)
        n1 = apply_layer_norm_axis1(xt).astype(jnp.bfloat16)
        hidden = jnp.maximum(
            jnp.einsum("kh,iks->ihs", homolog_widen_weights, n1, preferred_element_type=jnp.float32), 0.0
        ).astype(jnp.bfloat16)
        refreshed_t = (
            xt + jnp.einsum("hk,ihs->iks", homolog_shrink_weights, hidden, preferred_element_type=jnp.float32)
        ).astype(jnp.bfloat16)
        refreshed_parts.append(refreshed_t)
        n2 = apply_layer_norm_axis1(refreshed_t.astype(jnp.float32)).astype(jnp.bfloat16)
        right_parts.append(
            jnp.einsum("ke,iks->sie", rhs_projector, n2, preferred_element_type=jnp.float32)
            .astype(jnp.bfloat16)
            .reshape(homologs_local_share, step * proj_width)
        )
        lt_parts.append(
            jnp.einsum("kc,iks->cis", lhs_projector, n2, preferred_element_type=jnp.float32).astype(jnp.bfloat16)
        )
    homolog_refreshed = jnp.transpose(jnp.concatenate(refreshed_parts, axis=0), (2, 0, 1))
    lt = jnp.concatenate(lt_parts, axis=1).reshape(proj_width * sites_local_share, homologs_local_share)
    owners = lax.axis_size(("seq", "chan"))
    depth_total = float(homologs_local_share * owners)
    block_cols = coupling_embedding.shape[1]

    w_hi_f32 = lax.reduce_precision(moment_coupling_weights, exponent_bits=8, mantissa_bits=7)
    w_hi = w_hi_f32.astype(jnp.bfloat16)
    w_lo = (moment_coupling_weights - w_hi_f32).astype(jnp.bfloat16)
    nres = lax.axis_size("res")
    if nres == 2:
        r_other = [lax.ppermute(r, "res", [(0, 1), (1, 0)]) for r in right_parts]
        p_own = outer_project(lt, right_parts, w_hi, w_lo, 1.0 / depth_total)
        chunk = 2 * p_own.shape[0] // (lax.axis_size("seq") * lax.axis_size("chan"))
        part_own = chan_stage(p_own, chunk)
        p_other = outer_project(lt, r_other, w_hi, w_lo, 1.0 / depth_total)
        part_other = chan_stage(p_other, chunk)
        pair_update = seq_stage_blocks(part_own, part_other)
    else:
        r_all = lax.all_gather(jnp.concatenate(right_parts, axis=1), "res", axis=1, tiled=True)
        partial_value = outer_project(lt, [r_all], w_hi, w_lo, 1.0 / depth_total)
        pair_update = reduce_over_sequences(partial_value)
    nja_local = block_cols // JB
    pair_update = (
        pair_update.reshape(nja_local, sites_local_share, JB, pair_width)
        .transpose(1, 0, 2, 3)
        .reshape(sites_local_share * block_cols, pair_width)
    )
    pair_mid = coupling_embedding.reshape(sites_local_share * block_cols, pair_width) + pair_update
    pair_norm = apply_layer_norm(pair_mid).astype(jnp.bfloat16)
    pair_hidden = jnp.maximum(
        jnp.dot(pair_norm, coupling_widen_weights, preferred_element_type=jnp.float32), 0.0
    ).astype(jnp.bfloat16)
    coupling_refreshed = pair_mid + jnp.dot(
        pair_hidden, coupling_shrink_weights, preferred_element_type=jnp.float32
    )
    return (
        homolog_refreshed,
        coupling_refreshed.reshape(sites_local_share, block_cols, pair_width),
    )


def solution(mesh):
    return jax.shard_map(
        per_device,
        mesh=mesh,
        in_specs=(
            P(("groups", "seq", "chan"), "res", None),
            P(("groups", "res"), ("seq", "chan"), None),
            P(),
            P(),
            P(),
            P(),
            P(),
            P(),
            P(),
        ),
        out_specs=(
            P(("groups", "seq", "chan"), "res", None),
            P(("groups", "res"), ("seq", "chan"), None),
        ),
        check_vma=False,
    )
```

```python
import functools

import jax
import jax.numpy as jnp
from jax import lax
from jax.experimental import pallas as pl
from jax.experimental.pallas import tpu as pltpu
from jax.sharding import PartitionSpec as P


def apply_layer_norm(values):
    mean = jnp.mean(values, axis=-1, keepdims=True)
    centred = values - mean
    variance = jnp.mean(centred * centred, axis=-1, keepdims=True)
    return centred * lax.rsqrt(variance + 1e-05)


def apply_layer_norm_axis1(values):
    mean = jnp.mean(values, axis=1, keepdims=True)
    centred = values - mean
    variance = jnp.mean(centred * centred, axis=1, keepdims=True)
    return centred * lax.rsqrt(variance + 1e-05)


C_HI = 8
C_LO = 4
JB = 4


def outer_project_kernel(scale, nlt, nparts, *refs):
    lt_refs = refs[:nlt]
    r_refs = refs[nlt : nlt + nparts]
    wh_ref, wl_ref, o_ref, vh_ref, vl_ref = refs[nlt + nparts :]
    width = wh_ref.shape[0] // (C_HI * C_LO)
    rows_i = sum(t.shape[1] for t in lt_refs)
    lanes = JB * width
    nja = sum(r.shape[1] for r in r_refs) // lanes
    dd = wh_ref.shape[1]

    @pl.when(pl.program_id(0) == 0)
    def _build():
        vh_ref[...] = jnp.zeros_like(vh_ref)
        vl_ref[...] = jnp.zeros_like(vl_ref)
        for c_hi in range(C_HI):
            for c_lo in range(C_LO):
                src = (c_hi * C_LO + c_lo) * width
                for jb in range(JB):
                    row = c_lo * lanes + jb * width
                    vh_ref[c_hi, row : row + width, jb * dd : (jb + 1) * dd] = wh_ref[src : src + width, :]
                    vl_ref[c_hi, row : row + width, jb * dd : (jb + 1) * dd] = wl_ref[src : src + width, :]

    def rearrange(y):
        return jnp.concatenate(
            [
                jnp.concatenate(
                    [y[c_lo * rows_i : (c_lo + 1) * rows_i, ja * lanes : (ja + 1) * lanes] for c_lo in range(C_LO)],
                    axis=1,
                )
                for ja in range(nja)
            ],
            axis=0,
        )

    acc = jnp.zeros(o_ref.shape, jnp.float32)
    block = C_LO * rows_i
    for c_hi in range(C_HI):
        lt_blk = jnp.concatenate(
            [t[c_hi * C_LO + c_lo] for c_lo in range(C_LO) for t in lt_refs], axis=0
        )
        xs = [jnp.dot(lt_blk, r[...], preferred_element_type=jnp.float32) for r in r_refs]
        x = xs[0] if nparts == 1 else jnp.concatenate(xs, axis=1)
        xh = x.astype(jnp.bfloat16)
        xl = (x - xh.astype(jnp.float32)).astype(jnp.bfloat16)
        lh = rearrange(xh)
        ll = rearrange(xl)
        vh = vh_ref[c_hi]
        acc = acc + jnp.dot(lh, vh, preferred_element_type=jnp.float32)
        acc = acc + jnp.dot(ll, vh, preferred_element_type=jnp.float32)
        acc = acc + jnp.dot(lh, vl_ref[c_hi], preferred_element_type=jnp.float32)
    o_ref[...] = acc * scale


def outer_project(lt_parts, r_parts, wh, wl, scale):
    nparts = len(r_parts)
    nlt = len(lt_parts)
    r_all = r_parts[0]
    rows_i = sum(t.shape[1] for t in lt_parts)
    width = wh.shape[0] // (C_HI * C_LO)
    lanes = JB * width
    total_lanes = sum(r.shape[1] for r in r_parts)
    chunk = min(total_lanes, 16 * lanes)
    if nparts > 1:
        assert chunk == total_lanes
    steps = total_lanes // chunk
    nja_chunk = chunk // lanes
    out_rows = (total_lanes // lanes) * rows_i
    d = wh.shape[1]
    s = lt_parts[0].shape[2]
    flops = 2 * C_HI * C_LO * rows_i * s * total_lanes + 3 * 2 * out_rows * (C_LO * lanes) * (JB * d) * C_HI
    return pl.pallas_call(
        functools.partial(outer_project_kernel, scale, nlt, nparts),
        grid=(steps,),
        in_specs=[
            *[pl.BlockSpec(t.shape, lambda q: (0, 0, 0)) for t in lt_parts],
            *(
                [pl.BlockSpec((s, chunk), lambda q: (0, q))]
                if nparts == 1
                else [pl.BlockSpec(r.shape, lambda q: (0, 0)) for r in r_parts]
            ),
            pl.BlockSpec(wh.shape, lambda q: (0, 0)),
            pl.BlockSpec(wl.shape, lambda q: (0, 0)),
        ],
        out_specs=pl.BlockSpec((nja_chunk * rows_i, JB * d), lambda q: (q, 0)),
        out_shape=jax.ShapeDtypeStruct((out_rows, JB * d), jnp.float32),
        scratch_shapes=[
            pltpu.VMEM((C_HI, C_LO * lanes, JB * d), jnp.bfloat16),
            pltpu.VMEM((C_HI, C_LO * lanes, JB * d), jnp.bfloat16),
        ],
        compiler_params=pltpu.CompilerParams(
            dimension_semantics=("arbitrary",), vmem_limit_bytes=48 * 1024 * 1024
        ),
        cost_estimate=pl.CostEstimate(
            flops=flops,
            transcendentals=0,
            bytes_accessed=C_HI * C_LO * rows_i * s * 2 + total_lanes * s * 2 + wh.size * 4 + out_rows * JB * d * 4,
        ),
    )(*lt_parts, *r_parts, wh, wl)


def chan_stage(block, chunk):
    nchan = lax.axis_size("chan")
    rows, cols = block.shape
    xs = block.reshape(rows // (chunk * nchan), nchan, chunk, cols)
    c = lax.axis_index("chan")
    mine = lax.dynamic_index_in_dim(xs, c, axis=1, keepdims=False)
    other = lax.dynamic_index_in_dim(xs, 1 - c, axis=1, keepdims=False)
    return mine + lax.ppermute(other, "chan", [(0, 1), (1, 0)])


def seq_stage(part):
    nseq = lax.axis_size("seq")
    if nseq > 4:
        gathered = lax.all_to_all(part, "seq", 0, 0, tiled=False)
        return gathered.sum(axis=0)
    me = lax.axis_index("seq")
    acc = lax.dynamic_index_in_dim(part, me, axis=0, keepdims=False)
    for k in range(1, nseq):
        src = lax.dynamic_index_in_dim(part, (me + k) % nseq, axis=0, keepdims=False)
        acc = acc + lax.ppermute(src, "seq", [(q, (q + k) % nseq) for q in range(nseq)])
    return acc


def reduce_over_sequences(partial_value):
    if lax.axis_size("chan") != 2:
        return lax.psum_scatter(partial_value, ("seq", "chan"), scatter_dimension=0, tiled=True)
    chunk = partial_value.shape[0] // (lax.axis_size("seq") * lax.axis_size("chan"))
    return seq_stage(chan_stage(partial_value, chunk))


def per_device(
    homolog_embedding,
    coupling_embedding,
    homolog_widen_weights,
    homolog_shrink_weights,
    lhs_projector,
    rhs_projector,
    moment_coupling_weights,
    coupling_widen_weights,
    coupling_shrink_weights,
):
    homologs_local_share, sites_local_share, homolog_lane_number = homolog_embedding.shape
    proj_width = lhs_projector.shape[1]
    pair_width = coupling_embedding.shape[2]
    xt_all = jnp.transpose(homolog_embedding, (1, 2, 0))
    halves = 2 if sites_local_share % 16 == 0 else 1
    step = sites_local_share // halves
    refreshed_parts, lt_parts, right_parts = [], [], []
    for h in range(halves):
        xt = xt_all[h * step : (h + 1) * step].astype(jnp.float32)
        n1 = apply_layer_norm_axis1(xt).astype(jnp.bfloat16)
        hidden = jnp.maximum(
            jnp.einsum("kh,iks->ihs", homolog_widen_weights, n1, preferred_element_type=jnp.float32), 0.0
        ).astype(jnp.bfloat16)
        refreshed_t = (
            xt + jnp.einsum("hk,ihs->iks", homolog_shrink_weights, hidden, preferred_element_type=jnp.float32)
        ).astype(jnp.bfloat16)
        refreshed_parts.append(refreshed_t)
        n2 = apply_layer_norm_axis1(refreshed_t.astype(jnp.float32)).astype(jnp.bfloat16)
        right_parts.append(
            jnp.einsum("ke,iks->sie", rhs_projector, n2, preferred_element_type=jnp.float32)
            .astype(jnp.bfloat16)
            .reshape(homologs_local_share, step * proj_width)
        )
        lt_parts.append(
            jnp.einsum("kc,iks->cis", lhs_projector, n2, preferred_element_type=jnp.float32).astype(jnp.bfloat16)
        )
    homolog_refreshed = jnp.transpose(jnp.concatenate(refreshed_parts, axis=0), (2, 0, 1))
    owners = lax.axis_size(("seq", "chan"))
    depth_total = float(homologs_local_share * owners)
    block_cols = coupling_embedding.shape[1]

    w_hi_f32 = lax.reduce_precision(moment_coupling_weights, exponent_bits=8, mantissa_bits=7)
    w_hi = w_hi_f32.astype(jnp.bfloat16)
    w_lo = (moment_coupling_weights - w_hi_f32).astype(jnp.bfloat16)
    nres = lax.axis_size("res")
    if nres == 2:
        r_other = [lax.ppermute(r, "res", [(0, 1), (1, 0)]) for r in right_parts]
        p_own = outer_project(lt_parts, right_parts, w_hi, w_lo, 1.0 / depth_total)
        chunk = 2 * p_own.shape[0] // (lax.axis_size("seq") * lax.axis_size("chan"))
        part_own = chan_stage(p_own, chunk)
        p_other = outer_project(lt_parts, r_other, w_hi, w_lo, 1.0 / depth_total)
        part_other = chan_stage(p_other, chunk)
        first = lax.axis_index("res") == 0
        part = jnp.where(
            first, jnp.concatenate([part_own, part_other], axis=0), jnp.concatenate([part_other, part_own], axis=0)
        )
        pair_update = seq_stage(part)
    else:
        r_all = lax.all_gather(jnp.concatenate(right_parts, axis=1), "res", axis=1, tiled=True)
        partial_value = outer_project(lt_parts, [r_all], w_hi, w_lo, 1.0 / depth_total)
        pair_update = reduce_over_sequences(partial_value)
    nja_local = block_cols // JB
    pair_update = (
        pair_update.reshape(nja_local, sites_local_share, JB, pair_width)
        .transpose(1, 0, 2, 3)
        .reshape(sites_local_share * block_cols, pair_width)
    )
    pair_mid = coupling_embedding.reshape(sites_local_share * block_cols, pair_width) + pair_update
    pair_norm = apply_layer_norm(pair_mid).astype(jnp.bfloat16)
    pair_hidden = jnp.maximum(
        jnp.dot(pair_norm, coupling_widen_weights, preferred_element_type=jnp.float32), 0.0
    ).astype(jnp.bfloat16)
    coupling_refreshed = pair_mid + jnp.dot(
        pair_hidden, coupling_shrink_weights, preferred_element_type=jnp.float32
    )
    return (
        homolog_refreshed,
        coupling_refreshed.reshape(sites_local_share, block_cols, pair_width),
    )


def solution(mesh):
    return jax.shard_map(
        per_device,
        mesh=mesh,
        in_specs=(
            P(("groups", "seq", "chan"), "res", None),
            P(("groups", "res"), ("seq", "chan"), None),
            P(),
            P(),
            P(),
            P(),
            P(),
            P(),
            P(),
        ),
        out_specs=(
            P(("groups", "seq", "chan"), "res", None),
            P(("groups", "res"), ("seq", "chan"), None),
        ),
        check_vma=False,
    )
```

```python
import functools

import jax
import jax.numpy as jnp
from jax import lax
from jax.experimental import pallas as pl
from jax.experimental.pallas import tpu as pltpu
from jax.sharding import PartitionSpec as P


def apply_layer_norm(values):
    mean = jnp.mean(values, axis=-1, keepdims=True)
    centred = values - mean
    variance = jnp.mean(centred * centred, axis=-1, keepdims=True)
    return centred * lax.rsqrt(variance + 1e-05)


def apply_layer_norm_axis1(values):
    mean = jnp.mean(values, axis=1, keepdims=True)
    centred = values - mean
    variance = jnp.mean(centred * centred, axis=1, keepdims=True)
    return centred * lax.rsqrt(variance + 1e-05)


C_HI = 8
C_LO = 4
JB = 4


def outer_project_kernel(scale, nlt, nparts, *refs):
    lt_refs = refs[:nlt]
    r_refs = refs[nlt : nlt + nparts]
    wh_ref, wl_ref, o_ref, vh_ref, vl_ref = refs[nlt + nparts :]
    width = wh_ref.shape[0] // (C_HI * C_LO)
    rows_i = sum(t.shape[1] for t in lt_refs)
    lanes = JB * width
    nja = sum(r.shape[1] for r in r_refs) // lanes
    dd = wh_ref.shape[1]

    @pl.when(pl.program_id(0) == 0)
    def _build():
        vh_ref[...] = jnp.zeros_like(vh_ref)
        vl_ref[...] = jnp.zeros_like(vl_ref)
        for c_hi in range(C_HI):
            for c_lo in range(C_LO):
                src = (c_hi * C_LO + c_lo) * width
                for jb in range(JB):
                    row = c_lo * lanes + jb * width
                    vh_ref[c_hi, row : row + width, jb * dd : (jb + 1) * dd] = wh_ref[src : src + width, :]
                    vl_ref[c_hi, row : row + width, jb * dd : (jb + 1) * dd] = wl_ref[src : src + width, :]

    def rearrange(y):
        return jnp.concatenate(
            [
                jnp.concatenate(
                    [y[c_lo * rows_i : (c_lo + 1) * rows_i, ja * lanes : (ja + 1) * lanes] for c_lo in range(C_LO)],
                    axis=1,
                )
                for ja in range(nja)
            ],
            axis=0,
        )

    acc = jnp.zeros(o_ref.shape, jnp.float32)
    block = C_LO * rows_i
    for c_hi in range(C_HI):
        lt_blk = jnp.concatenate(
            [t[c_hi * C_LO + c_lo] for c_lo in range(C_LO) for t in lt_refs], axis=0
        )
        xs = [jnp.dot(lt_blk, r[...], preferred_element_type=jnp.float32) for r in r_refs]
        x = xs[0] if nparts == 1 else jnp.concatenate(xs, axis=1)
        xh = x.astype(jnp.bfloat16)
        xl = (x - xh.astype(jnp.float32)).astype(jnp.bfloat16)
        lh = rearrange(xh)
        ll = rearrange(xl)
        vh = vh_ref[c_hi]
        acc = acc + jnp.dot(lh, vh, preferred_element_type=jnp.float32)
        acc = acc + jnp.dot(ll, vh, preferred_element_type=jnp.float32)
        acc = acc + jnp.dot(lh, vl_ref[c_hi], preferred_element_type=jnp.float32)
    o_ref[...] = acc * scale


def outer_project(lt_parts, r_parts, wh, wl, scale):
    nparts = len(r_parts)
    nlt = len(lt_parts)
    r_all = r_parts[0]
    rows_i = sum(t.shape[1] for t in lt_parts)
    width = wh.shape[0] // (C_HI * C_LO)
    lanes = JB * width
    total_lanes = sum(r.shape[1] for r in r_parts)
    chunk = min(total_lanes, 16 * lanes)
    if nparts > 1:
        assert chunk == total_lanes
    steps = total_lanes // chunk
    nja_chunk = chunk // lanes
    out_rows = (total_lanes // lanes) * rows_i
    d = wh.shape[1]
    s = lt_parts[0].shape[2]
    flops = 2 * C_HI * C_LO * rows_i * s * total_lanes + 3 * 2 * out_rows * (C_LO * lanes) * (JB * d) * C_HI
    return pl.pallas_call(
        functools.partial(outer_project_kernel, scale, nlt, nparts),
        grid=(steps,),
        in_specs=[
            *[pl.BlockSpec(t.shape, lambda q: (0, 0, 0)) for t in lt_parts],
            *(
                [pl.BlockSpec((s, chunk), lambda q: (0, q))]
                if nparts == 1
                else [pl.BlockSpec(r.shape, lambda q: (0, 0)) for r in r_parts]
            ),
            pl.BlockSpec(wh.shape, lambda q: (0, 0)),
            pl.BlockSpec(wl.shape, lambda q: (0, 0)),
        ],
        out_specs=pl.BlockSpec((nja_chunk * rows_i, JB * d), lambda q: (q, 0)),
        out_shape=jax.ShapeDtypeStruct((out_rows, JB * d), jnp.float32),
        scratch_shapes=[
            pltpu.VMEM((C_HI, C_LO * lanes, JB * d), jnp.bfloat16),
            pltpu.VMEM((C_HI, C_LO * lanes, JB * d), jnp.bfloat16),
        ],
        compiler_params=pltpu.CompilerParams(
            dimension_semantics=("arbitrary",), vmem_limit_bytes=48 * 1024 * 1024
        ),
        cost_estimate=pl.CostEstimate(
            flops=flops,
            transcendentals=0,
            bytes_accessed=C_HI * C_LO * rows_i * s * 2 + total_lanes * s * 2 + wh.size * 4 + out_rows * JB * d * 4,
        ),
    )(*lt_parts, *r_parts, wh, wl)


def chan_stage(block, chunk):
    nchan = lax.axis_size("chan")
    rows, cols = block.shape
    xs = block.reshape(rows // (chunk * nchan), nchan, chunk, cols)
    c = lax.axis_index("chan")
    mine = lax.dynamic_index_in_dim(xs, c, axis=1, keepdims=False)
    other = lax.dynamic_index_in_dim(xs, 1 - c, axis=1, keepdims=False)
    return mine + lax.ppermute(other, "chan", [(0, 1), (1, 0)])


def seq_stage(part):
    nseq = lax.axis_size("seq")
    if nseq > 4:
        gathered = lax.all_to_all(part, "seq", 0, 0, tiled=False)
        return gathered.sum(axis=0)
    me = lax.axis_index("seq")
    if nseq == 4:
        pairs = part.reshape(2, 2, *part.shape[1:])
        lo = me % 2
        keep = lax.dynamic_index_in_dim(pairs, lo, axis=1, keepdims=False)
        send = lax.dynamic_index_in_dim(pairs, 1 - lo, axis=1, keepdims=False)
        half = keep + lax.ppermute(send, "seq", [(q, q ^ 1) for q in range(4)])
        hi = me // 2
        keep2 = lax.dynamic_index_in_dim(half, hi, axis=0, keepdims=False)
        send2 = lax.dynamic_index_in_dim(half, 1 - hi, axis=0, keepdims=False)
        return keep2 + lax.ppermute(send2, "seq", [(q, q ^ 2) for q in range(4)])
    acc = lax.dynamic_index_in_dim(part, me, axis=0, keepdims=False)
    for k in range(1, nseq):
        src = lax.dynamic_index_in_dim(part, (me + k) % nseq, axis=0, keepdims=False)
        acc = acc + lax.ppermute(src, "seq", [(q, (q + k) % nseq) for q in range(nseq)])
    return acc


def reduce_over_sequences(partial_value):
    if lax.axis_size("chan") != 2:
        return lax.psum_scatter(partial_value, ("seq", "chan"), scatter_dimension=0, tiled=True)
    chunk = partial_value.shape[0] // (lax.axis_size("seq") * lax.axis_size("chan"))
    return seq_stage(chan_stage(partial_value, chunk))


def per_device(
    homolog_embedding,
    coupling_embedding,
    homolog_widen_weights,
    homolog_shrink_weights,
    lhs_projector,
    rhs_projector,
    moment_coupling_weights,
    coupling_widen_weights,
    coupling_shrink_weights,
):
    homologs_local_share, sites_local_share, homolog_lane_number = homolog_embedding.shape
    proj_width = lhs_projector.shape[1]
    pair_width = coupling_embedding.shape[2]
    xt_all = jnp.transpose(homolog_embedding, (1, 2, 0))
    halves = 2 if sites_local_share % 16 == 0 else 1
    step = sites_local_share // halves
    refreshed_parts, lt_parts, right_parts = [], [], []
    for h in range(halves):
        xt = xt_all[h * step : (h + 1) * step].astype(jnp.float32)
        n1 = apply_layer_norm_axis1(xt).astype(jnp.bfloat16)
        hidden = jnp.maximum(
            jnp.einsum("kh,iks->ihs", homolog_widen_weights, n1, preferred_element_type=jnp.float32), 0.0
        ).astype(jnp.bfloat16)
        refreshed_t = (
            xt + jnp.einsum("hk,ihs->iks", homolog_shrink_weights, hidden, preferred_element_type=jnp.float32)
        ).astype(jnp.bfloat16)
        refreshed_parts.append(refreshed_t)
        n2 = apply_layer_norm_axis1(refreshed_t.astype(jnp.float32)).astype(jnp.bfloat16)
        right_parts.append(
            jnp.einsum("ke,iks->sie", rhs_projector, n2, preferred_element_type=jnp.float32)
            .astype(jnp.bfloat16)
            .reshape(homologs_local_share, step * proj_width)
        )
        lt_parts.append(
            jnp.einsum("kc,iks->cis", lhs_projector, n2, preferred_element_type=jnp.float32).astype(jnp.bfloat16)
        )
    homolog_refreshed = jnp.transpose(jnp.concatenate(refreshed_parts, axis=0), (2, 0, 1))
    owners = lax.axis_size(("seq", "chan"))
    depth_total = float(homologs_local_share * owners)
    block_cols = coupling_embedding.shape[1]

    w_hi_f32 = lax.reduce_precision(moment_coupling_weights, exponent_bits=8, mantissa_bits=7)
    w_hi = w_hi_f32.astype(jnp.bfloat16)
    w_lo = (moment_coupling_weights - w_hi_f32).astype(jnp.bfloat16)
    nres = lax.axis_size("res")
    if nres == 2:
        r_other = [lax.ppermute(r, "res", [(0, 1), (1, 0)]) for r in right_parts]
        p_own = outer_project(lt_parts, right_parts, w_hi, w_lo, 1.0 / depth_total)
        chunk = 2 * p_own.shape[0] // (lax.axis_size("seq") * lax.axis_size("chan"))
        part_own = chan_stage(p_own, chunk)
        p_other = outer_project(lt_parts, r_other, w_hi, w_lo, 1.0 / depth_total)
        part_other = chan_stage(p_other, chunk)
        first = lax.axis_index("res") == 0
        part = jnp.where(
            first, jnp.concatenate([part_own, part_other], axis=0), jnp.concatenate([part_other, part_own], axis=0)
        )
        pair_update = seq_stage(part)
    else:
        r_all = lax.all_gather(jnp.concatenate(right_parts, axis=1), "res", axis=1, tiled=True)
        partial_value = outer_project(lt_parts, [r_all], w_hi, w_lo, 1.0 / depth_total)
        pair_update = reduce_over_sequences(partial_value)
    nja_local = block_cols // JB
    pair_update = (
        pair_update.reshape(nja_local, sites_local_share, JB, pair_width)
        .transpose(1, 0, 2, 3)
        .reshape(sites_local_share * block_cols, pair_width)
    )
    pair_mid = coupling_embedding.reshape(sites_local_share * block_cols, pair_width) + pair_update
    pair_norm = apply_layer_norm(pair_mid).astype(jnp.bfloat16)
    pair_hidden = jnp.maximum(
        jnp.dot(pair_norm, coupling_widen_weights, preferred_element_type=jnp.float32), 0.0
    ).astype(jnp.bfloat16)
    coupling_refreshed = pair_mid + jnp.dot(
        pair_hidden, coupling_shrink_weights, preferred_element_type=jnp.float32
    )
    return (
        homolog_refreshed,
        coupling_refreshed.reshape(sites_local_share, block_cols, pair_width),
    )


def solution(mesh):
    return jax.shard_map(
        per_device,
        mesh=mesh,
        in_specs=(
            P(("groups", "seq", "chan"), "res", None),
            P(("groups", "res"), ("seq", "chan"), None),
            P(),
            P(),
            P(),
            P(),
            P(),
            P(),
            P(),
        ),
        out_specs=(
            P(("groups", "seq", "chan"), "res", None),
            P(("groups", "res"), ("seq", "chan"), None),
        ),
        check_vma=False,
    )
```

```python
import functools

import jax
import jax.numpy as jnp
from jax import lax
from jax.experimental import pallas as pl
from jax.experimental.pallas import tpu as pltpu
from jax.sharding import PartitionSpec as P


def apply_layer_norm(values):
    mean = jnp.mean(values, axis=-1, keepdims=True)
    centred = values - mean
    variance = jnp.mean(centred * centred, axis=-1, keepdims=True)
    return centred * lax.rsqrt(variance + 1e-05)


def apply_layer_norm_axis1(values):
    mean = jnp.mean(values, axis=1, keepdims=True)
    centred = values - mean
    variance = jnp.mean(centred * centred, axis=1, keepdims=True)
    return centred * lax.rsqrt(variance + 1e-05)


C_HI = 8
C_LO = 4
JB = 4


def outer_project_kernel(scale, nlt, nparts, *refs):
    lt_refs = refs[:nlt]
    r_refs = refs[nlt : nlt + nparts]
    wh_ref, wl_ref, o_ref, vh_ref, vl_ref = refs[nlt + nparts :]
    width = wh_ref.shape[0] // (C_HI * C_LO)
    rows_i = sum(t.shape[1] for t in lt_refs)
    lanes = JB * width
    nja = sum(r.shape[1] for r in r_refs) // lanes
    dd = wh_ref.shape[1]

    @pl.when(pl.program_id(0) == 0)
    def _build():
        vh_ref[...] = jnp.zeros_like(vh_ref)
        vl_ref[...] = jnp.zeros_like(vl_ref)
        for c_hi in range(C_HI):
            for c_lo in range(C_LO):
                src = (c_hi * C_LO + c_lo) * width
                for jb in range(JB):
                    row = c_lo * lanes + jb * width
                    vh_ref[c_hi, row : row + width, jb * dd : (jb + 1) * dd] = wh_ref[src : src + width, :]
                    vl_ref[c_hi, row : row + width, jb * dd : (jb + 1) * dd] = wl_ref[src : src + width, :]

    def rearrange(y):
        return jnp.concatenate(
            [
                jnp.concatenate(
                    [y[c_lo * rows_i : (c_lo + 1) * rows_i, ja * lanes : (ja + 1) * lanes] for c_lo in range(C_LO)],
                    axis=1,
                )
                for ja in range(nja)
            ],
            axis=0,
        )

    acc = jnp.zeros(o_ref.shape, jnp.float32)
    block = C_LO * rows_i
    lt_all = jnp.concatenate([t[c] for c in range(C_HI * C_LO) for t in lt_refs], axis=0)
    xs = [jnp.dot(lt_all, r[...], preferred_element_type=jnp.float32) for r in r_refs]
    x_all = xs[0] if nparts == 1 else jnp.concatenate(xs, axis=1)
    n = acc.shape[0]
    for c_hi in range(C_HI):
        x = x_all[c_hi * block : (c_hi + 1) * block]
        xh = x.astype(jnp.bfloat16)
        xl = (x - xh.astype(jnp.float32)).astype(jnp.bfloat16)
        lh = rearrange(xh)
        ll = rearrange(xl)
        both = jnp.dot(jnp.concatenate([lh, ll], axis=0), vh_ref[c_hi], preferred_element_type=jnp.float32)
        acc = acc + both[:n]
        acc = acc + both[n:]
        acc = acc + jnp.dot(lh, vl_ref[c_hi], preferred_element_type=jnp.float32)
    o_ref[...] = acc * scale


def outer_project(lt_parts, r_parts, wh, wl, scale):
    nparts = len(r_parts)
    nlt = len(lt_parts)
    r_all = r_parts[0]
    rows_i = sum(t.shape[1] for t in lt_parts)
    width = wh.shape[0] // (C_HI * C_LO)
    lanes = JB * width
    total_lanes = sum(r.shape[1] for r in r_parts)
    chunk = min(total_lanes, 16 * lanes)
    if nparts > 1:
        assert chunk == total_lanes
    steps = total_lanes // chunk
    nja_chunk = chunk // lanes
    out_rows = (total_lanes // lanes) * rows_i
    d = wh.shape[1]
    s = lt_parts[0].shape[2]
    flops = 2 * C_HI * C_LO * rows_i * s * total_lanes + 3 * 2 * out_rows * (C_LO * lanes) * (JB * d) * C_HI
    return pl.pallas_call(
        functools.partial(outer_project_kernel, scale, nlt, nparts),
        grid=(steps,),
        in_specs=[
            *[pl.BlockSpec(t.shape, lambda q: (0, 0, 0)) for t in lt_parts],
            *(
                [pl.BlockSpec((s, chunk), lambda q: (0, q))]
                if nparts == 1
                else [pl.BlockSpec(r.shape, lambda q: (0, 0)) for r in r_parts]
            ),
            pl.BlockSpec(wh.shape, lambda q: (0, 0)),
            pl.BlockSpec(wl.shape, lambda q: (0, 0)),
        ],
        out_specs=pl.BlockSpec((nja_chunk * rows_i, JB * d), lambda q: (q, 0)),
        out_shape=jax.ShapeDtypeStruct((out_rows, JB * d), jnp.float32),
        scratch_shapes=[
            pltpu.VMEM((C_HI, C_LO * lanes, JB * d), jnp.bfloat16),
            pltpu.VMEM((C_HI, C_LO * lanes, JB * d), jnp.bfloat16),
        ],
        compiler_params=pltpu.CompilerParams(
            dimension_semantics=("arbitrary",), vmem_limit_bytes=48 * 1024 * 1024
        ),
        cost_estimate=pl.CostEstimate(
            flops=flops,
            transcendentals=0,
            bytes_accessed=C_HI * C_LO * rows_i * s * 2 + total_lanes * s * 2 + wh.size * 4 + out_rows * JB * d * 4,
        ),
    )(*lt_parts, *r_parts, wh, wl)


def chan_stage(block, chunk):
    nchan = lax.axis_size("chan")
    rows, cols = block.shape
    xs = block.reshape(rows // (chunk * nchan), nchan, chunk, cols)
    c = lax.axis_index("chan")
    mine = lax.dynamic_index_in_dim(xs, c, axis=1, keepdims=False)
    other = lax.dynamic_index_in_dim(xs, 1 - c, axis=1, keepdims=False)
    return mine + lax.ppermute(other, "chan", [(0, 1), (1, 0)])


def seq_stage(part):
    nseq = lax.axis_size("seq")
    if nseq > 4:
        gathered = lax.all_to_all(part, "seq", 0, 0, tiled=False)
        return gathered.sum(axis=0)
    me = lax.axis_index("seq")
    acc = lax.dynamic_index_in_dim(part, me, axis=0, keepdims=False)
    for k in range(1, nseq):
        src = lax.dynamic_index_in_dim(part, (me + k) % nseq, axis=0, keepdims=False)
        acc = acc + lax.ppermute(src, "seq", [(q, (q + k) % nseq) for q in range(nseq)])
    return acc


def reduce_over_sequences(partial_value):
    if lax.axis_size("chan") != 2:
        return lax.psum_scatter(partial_value, ("seq", "chan"), scatter_dimension=0, tiled=True)
    chunk = partial_value.shape[0] // (lax.axis_size("seq") * lax.axis_size("chan"))
    return seq_stage(chan_stage(partial_value, chunk))


def per_device(
    homolog_embedding,
    coupling_embedding,
    homolog_widen_weights,
    homolog_shrink_weights,
    lhs_projector,
    rhs_projector,
    moment_coupling_weights,
    coupling_widen_weights,
    coupling_shrink_weights,
):
    homologs_local_share, sites_local_share, homolog_lane_number = homolog_embedding.shape
    proj_width = lhs_projector.shape[1]
    pair_width = coupling_embedding.shape[2]
    xt_all = jnp.transpose(homolog_embedding, (1, 2, 0))
    halves = 2 if sites_local_share % 16 == 0 else 1
    step = sites_local_share // halves
    refreshed_parts, lt_parts, right_parts = [], [], []
    for h in range(halves):
        xt = xt_all[h * step : (h + 1) * step].astype(jnp.float32)
        n1 = apply_layer_norm_axis1(xt).astype(jnp.bfloat16)
        hidden = jnp.maximum(
            jnp.einsum("kh,iks->ihs", homolog_widen_weights, n1, preferred_element_type=jnp.float32), 0.0
        ).astype(jnp.bfloat16)
        refreshed_t = (
            xt + jnp.einsum("hk,ihs->iks", homolog_shrink_weights, hidden, preferred_element_type=jnp.float32)
        ).astype(jnp.bfloat16)
        refreshed_parts.append(refreshed_t)
        n2 = apply_layer_norm_axis1(refreshed_t.astype(jnp.float32)).astype(jnp.bfloat16)
        right_parts.append(
            jnp.einsum("ke,iks->sie", rhs_projector, n2, preferred_element_type=jnp.float32)
            .astype(jnp.bfloat16)
            .reshape(homologs_local_share, step * proj_width)
        )
        lt_parts.append(
            jnp.einsum("kc,iks->cis", lhs_projector, n2, preferred_element_type=jnp.float32).astype(jnp.bfloat16)
        )
    homolog_refreshed = jnp.transpose(jnp.concatenate(refreshed_parts, axis=0), (2, 0, 1))
    owners = lax.axis_size(("seq", "chan"))
    depth_total = float(homologs_local_share * owners)
    block_cols = coupling_embedding.shape[1]

    w_hi_f32 = lax.reduce_precision(moment_coupling_weights, exponent_bits=8, mantissa_bits=7)
    w_hi = w_hi_f32.astype(jnp.bfloat16)
    w_lo = (moment_coupling_weights - w_hi_f32).astype(jnp.bfloat16)
    nres = lax.axis_size("res")
    if nres == 2:
        r_other = [lax.ppermute(r, "res", [(0, 1), (1, 0)]) for r in right_parts]
        p_own = outer_project(lt_parts, right_parts, w_hi, w_lo, 1.0 / depth_total)
        chunk = 2 * p_own.shape[0] // (lax.axis_size("seq") * lax.axis_size("chan"))
        part_own = chan_stage(p_own, chunk)
        p_other = outer_project(lt_parts, r_other, w_hi, w_lo, 1.0 / depth_total)
        part_other = chan_stage(p_other, chunk)
        first = lax.axis_index("res") == 0
        part = jnp.where(
            first, jnp.concatenate([part_own, part_other], axis=0), jnp.concatenate([part_other, part_own], axis=0)
        )
        pair_update = seq_stage(part)
    else:
        r_all = lax.all_gather(jnp.concatenate(right_parts, axis=1), "res", axis=1, tiled=True)
        partial_value = outer_project(lt_parts, [r_all], w_hi, w_lo, 1.0 / depth_total)
        pair_update = reduce_over_sequences(partial_value)
    nja_local = block_cols // JB
    pair_update = (
        pair_update.reshape(nja_local, sites_local_share, JB, pair_width)
        .transpose(1, 0, 2, 3)
        .reshape(sites_local_share * block_cols, pair_width)
    )
    pair_mid = coupling_embedding.reshape(sites_local_share * block_cols, pair_width) + pair_update
    pair_norm = apply_layer_norm(pair_mid).astype(jnp.bfloat16)
    pair_hidden = jnp.maximum(
        jnp.dot(pair_norm, coupling_widen_weights, preferred_element_type=jnp.float32), 0.0
    ).astype(jnp.bfloat16)
    coupling_refreshed = pair_mid + jnp.dot(
        pair_hidden, coupling_shrink_weights, preferred_element_type=jnp.float32
    )
    return (
        homolog_refreshed,
        coupling_refreshed.reshape(sites_local_share, block_cols, pair_width),
    )


def solution(mesh):
    return jax.shard_map(
        per_device,
        mesh=mesh,
        in_specs=(
            P(("groups", "seq", "chan"), "res", None),
            P(("groups", "res"), ("seq", "chan"), None),
            P(),
            P(),
            P(),
            P(),
            P(),
            P(),
            P(),
        ),
        out_specs=(
            P(("groups", "seq", "chan"), "res", None),
            P(("groups", "res"), ("seq", "chan"), None),
        ),
        check_vma=False,
    )
```

```python
import functools

import jax
import jax.numpy as jnp
from jax import lax
from jax.experimental import pallas as pl
from jax.experimental.pallas import tpu as pltpu
from jax.sharding import PartitionSpec as P


def apply_layer_norm(values):
    mean = jnp.mean(values, axis=-1, keepdims=True)
    centred = values - mean
    variance = jnp.mean(centred * centred, axis=-1, keepdims=True)
    return centred * lax.rsqrt(variance + 1e-05)


def apply_layer_norm_axis1(values):
    mean = jnp.mean(values, axis=1, keepdims=True)
    centred = values - mean
    variance = jnp.mean(centred * centred, axis=1, keepdims=True)
    return centred * lax.rsqrt(variance + 1e-05)


C_HI = 8
C_LO = 4
JB = 4


def outer_project_kernel(scale, nlt, nparts, *refs):
    lt_refs = refs[:nlt]
    r_refs = refs[nlt : nlt + nparts]
    wh_ref, wl_ref, o_ref, vh_ref, vl_ref = refs[nlt + nparts :]
    width = wh_ref.shape[0] // (C_HI * C_LO)
    rows_i = sum(t.shape[1] for t in lt_refs)
    lanes = JB * width
    nja = sum(r.shape[1] for r in r_refs) // lanes
    dd = wh_ref.shape[1]

    @pl.when(pl.program_id(0) == 0)
    def _build():
        vh_ref[...] = jnp.zeros_like(vh_ref)
        vl_ref[...] = jnp.zeros_like(vl_ref)
        for c_hi in range(C_HI):
            for c_lo in range(C_LO):
                src = (c_hi * C_LO + c_lo) * width
                for jb in range(JB):
                    row = c_lo * lanes + jb * width
                    vh_ref[c_hi, row : row + width, jb * dd : (jb + 1) * dd] = wh_ref[src : src + width, :]
                    vl_ref[c_hi, row : row + width, jb * dd : (jb + 1) * dd] = wl_ref[src : src + width, :]

    def rearrange(y):
        return jnp.concatenate(
            [
                jnp.concatenate(
                    [y[c_lo * rows_i : (c_lo + 1) * rows_i, ja * lanes : (ja + 1) * lanes] for c_lo in range(C_LO)],
                    axis=1,
                )
                for ja in range(nja)
            ],
            axis=0,
        )

    acc = jnp.zeros(o_ref.shape, jnp.float32)
    block = C_LO * rows_i
    lt_all = jnp.concatenate([t[c] for c in range(C_HI * C_LO) for t in lt_refs], axis=0)
    xs = [jnp.dot(lt_all, r[...], preferred_element_type=jnp.float32) for r in r_refs]
    x_all = xs[0] if nparts == 1 else jnp.concatenate(xs, axis=1)
    n = acc.shape[0]
    lhs_hi, lhs_lo = [], []
    for c_hi in range(C_HI):
        x = x_all[c_hi * block : (c_hi + 1) * block]
        xh = x.astype(jnp.bfloat16)
        xl = (x - xh.astype(jnp.float32)).astype(jnp.bfloat16)
        lhs_hi.append(rearrange(xh))
        lhs_lo.append(rearrange(xl))
    lh = jnp.concatenate(lhs_hi, axis=1)
    ll = jnp.concatenate(lhs_lo, axis=1)
    vh = vh_ref[...].reshape(C_HI * vh_ref.shape[1], vh_ref.shape[2])
    vl = vl_ref[...].reshape(C_HI * vl_ref.shape[1], vl_ref.shape[2])
    both = jnp.dot(jnp.concatenate([lh, ll], axis=0), vh, preferred_element_type=jnp.float32)
    acc = both[:n] + both[n:]
    acc = acc + jnp.dot(lh, vl, preferred_element_type=jnp.float32)
    o_ref[...] = acc * scale


def outer_project(lt_parts, r_parts, wh, wl, scale):
    nparts = len(r_parts)
    nlt = len(lt_parts)
    r_all = r_parts[0]
    rows_i = sum(t.shape[1] for t in lt_parts)
    width = wh.shape[0] // (C_HI * C_LO)
    lanes = JB * width
    total_lanes = sum(r.shape[1] for r in r_parts)
    chunk = min(total_lanes, 16 * lanes)
    if nparts > 1:
        assert chunk == total_lanes
    steps = total_lanes // chunk
    nja_chunk = chunk // lanes
    out_rows = (total_lanes // lanes) * rows_i
    d = wh.shape[1]
    s = lt_parts[0].shape[2]
    flops = 2 * C_HI * C_LO * rows_i * s * total_lanes + 3 * 2 * out_rows * (C_LO * lanes) * (JB * d) * C_HI
    return pl.pallas_call(
        functools.partial(outer_project_kernel, scale, nlt, nparts),
        grid=(steps,),
        in_specs=[
            *[pl.BlockSpec(t.shape, lambda q: (0, 0, 0)) for t in lt_parts],
            *(
                [pl.BlockSpec((s, chunk), lambda q: (0, q))]
                if nparts == 1
                else [pl.BlockSpec(r.shape, lambda q: (0, 0)) for r in r_parts]
            ),
            pl.BlockSpec(wh.shape, lambda q: (0, 0)),
            pl.BlockSpec(wl.shape, lambda q: (0, 0)),
        ],
        out_specs=pl.BlockSpec((nja_chunk * rows_i, JB * d), lambda q: (q, 0)),
        out_shape=jax.ShapeDtypeStruct((out_rows, JB * d), jnp.float32),
        scratch_shapes=[
            pltpu.VMEM((C_HI, C_LO * lanes, JB * d), jnp.bfloat16),
            pltpu.VMEM((C_HI, C_LO * lanes, JB * d), jnp.bfloat16),
        ],
        compiler_params=pltpu.CompilerParams(
            dimension_semantics=("arbitrary",), vmem_limit_bytes=48 * 1024 * 1024
        ),
        cost_estimate=pl.CostEstimate(
            flops=flops,
            transcendentals=0,
            bytes_accessed=C_HI * C_LO * rows_i * s * 2 + total_lanes * s * 2 + wh.size * 4 + out_rows * JB * d * 4,
        ),
    )(*lt_parts, *r_parts, wh, wl)


def chan_stage(block, chunk):
    nchan = lax.axis_size("chan")
    rows, cols = block.shape
    xs = block.reshape(rows // (chunk * nchan), nchan, chunk, cols)
    c = lax.axis_index("chan")
    mine = lax.dynamic_index_in_dim(xs, c, axis=1, keepdims=False)
    other = lax.dynamic_index_in_dim(xs, 1 - c, axis=1, keepdims=False)
    return mine + lax.ppermute(other, "chan", [(0, 1), (1, 0)])


def seq_stage(part):
    nseq = lax.axis_size("seq")
    if nseq > 4:
        gathered = lax.all_to_all(part, "seq", 0, 0, tiled=False)
        return gathered.sum(axis=0)
    me = lax.axis_index("seq")
    acc = lax.dynamic_index_in_dim(part, me, axis=0, keepdims=False)
    for k in range(1, nseq):
        src = lax.dynamic_index_in_dim(part, (me + k) % nseq, axis=0, keepdims=False)
        acc = acc + lax.ppermute(src, "seq", [(q, (q + k) % nseq) for q in range(nseq)])
    return acc


def reduce_over_sequences(partial_value):
    if lax.axis_size("chan") != 2:
        return lax.psum_scatter(partial_value, ("seq", "chan"), scatter_dimension=0, tiled=True)
    chunk = partial_value.shape[0] // (lax.axis_size("seq") * lax.axis_size("chan"))
    return seq_stage(chan_stage(partial_value, chunk))


def per_device(
    homolog_embedding,
    coupling_embedding,
    homolog_widen_weights,
    homolog_shrink_weights,
    lhs_projector,
    rhs_projector,
    moment_coupling_weights,
    coupling_widen_weights,
    coupling_shrink_weights,
):
    homologs_local_share, sites_local_share, homolog_lane_number = homolog_embedding.shape
    proj_width = lhs_projector.shape[1]
    pair_width = coupling_embedding.shape[2]
    xt_all = jnp.transpose(homolog_embedding, (1, 2, 0))
    halves = 2 if sites_local_share % 16 == 0 else 1
    step = sites_local_share // halves
    refreshed_parts, lt_parts, right_parts = [], [], []
    for h in range(halves):
        xt = xt_all[h * step : (h + 1) * step].astype(jnp.float32)
        n1 = apply_layer_norm_axis1(xt).astype(jnp.bfloat16)
        hidden = jnp.maximum(
            jnp.einsum("kh,iks->ihs", homolog_widen_weights, n1, preferred_element_type=jnp.float32), 0.0
        ).astype(jnp.bfloat16)
        refreshed_t = (
            xt + jnp.einsum("hk,ihs->iks", homolog_shrink_weights, hidden, preferred_element_type=jnp.float32)
        ).astype(jnp.bfloat16)
        refreshed_parts.append(refreshed_t)
        n2 = apply_layer_norm_axis1(refreshed_t.astype(jnp.float32)).astype(jnp.bfloat16)
        right_parts.append(
            jnp.einsum("ke,iks->sie", rhs_projector, n2, preferred_element_type=jnp.float32)
            .astype(jnp.bfloat16)
            .reshape(homologs_local_share, step * proj_width)
        )
        lt_parts.append(
            jnp.einsum("kc,iks->cis", lhs_projector, n2, preferred_element_type=jnp.float32).astype(jnp.bfloat16)
        )
    homolog_refreshed = jnp.transpose(jnp.concatenate(refreshed_parts, axis=0), (2, 0, 1))
    owners = lax.axis_size(("seq", "chan"))
    depth_total = float(homologs_local_share * owners)
    block_cols = coupling_embedding.shape[1]

    w_hi_f32 = lax.reduce_precision(moment_coupling_weights, exponent_bits=8, mantissa_bits=7)
    w_hi = w_hi_f32.astype(jnp.bfloat16)
    w_lo = (moment_coupling_weights - w_hi_f32).astype(jnp.bfloat16)
    nres = lax.axis_size("res")
    if nres == 2:
        r_other = [lax.ppermute(r, "res", [(0, 1), (1, 0)]) for r in right_parts]
        p_own = outer_project(lt_parts, right_parts, w_hi, w_lo, 1.0 / depth_total)
        chunk = 2 * p_own.shape[0] // (lax.axis_size("seq") * lax.axis_size("chan"))
        part_own = chan_stage(p_own, chunk)
        p_other = outer_project(lt_parts, r_other, w_hi, w_lo, 1.0 / depth_total)
        part_other = chan_stage(p_other, chunk)
        first = lax.axis_index("res") == 0
        part = jnp.where(
            first, jnp.concatenate([part_own, part_other], axis=0), jnp.concatenate([part_other, part_own], axis=0)
        )
        pair_update = seq_stage(part)
    else:
        r_all = lax.all_gather(jnp.concatenate(right_parts, axis=1), "res", axis=1, tiled=True)
        partial_value = outer_project(lt_parts, [r_all], w_hi, w_lo, 1.0 / depth_total)
        pair_update = reduce_over_sequences(partial_value)
    nja_local = block_cols // JB
    pair_update = (
        pair_update.reshape(nja_local, sites_local_share, JB, pair_width)
        .transpose(1, 0, 2, 3)
        .reshape(sites_local_share * block_cols, pair_width)
    )
    pair_mid = coupling_embedding.reshape(sites_local_share * block_cols, pair_width) + pair_update
    pair_norm = apply_layer_norm(pair_mid).astype(jnp.bfloat16)
    pair_hidden = jnp.maximum(
        jnp.dot(pair_norm, coupling_widen_weights, preferred_element_type=jnp.float32), 0.0
    ).astype(jnp.bfloat16)
    coupling_refreshed = pair_mid + jnp.dot(
        pair_hidden, coupling_shrink_weights, preferred_element_type=jnp.float32
    )
    return (
        homolog_refreshed,
        coupling_refreshed.reshape(sites_local_share, block_cols, pair_width),
    )


def solution(mesh):
    return jax.shard_map(
        per_device,
        mesh=mesh,
        in_specs=(
            P(("groups", "seq", "chan"), "res", None),
            P(("groups", "res"), ("seq", "chan"), None),
            P(),
            P(),
            P(),
            P(),
            P(),
            P(),
            P(),
        ),
        out_specs=(
            P(("groups", "seq", "chan"), "res", None),
            P(("groups", "res"), ("seq", "chan"), None),
        ),
        check_vma=False,
    )
```
